128 devices in a mesh: fold: 16 (over x, z), blk: 8 (over y, core).
Axes of the slice: x: 4, y: 4, z: 4, core: 2. Of those that a mesh axis runs over, the one named last changes fastest.
Arguments:
- genotypes: bfloat16 [131072, 8192], P('fold', 'blk'), may hold values from 0 to 2, as said below
- phenotypes: bfloat16 [32, 131072], P(None, 'fold'), may hold values from -4 to 4
- trait_order: int32 [32], replicated, may hold values from 0 to 31, each once
Outputs:
- predict: float32 [32, 131072], P('blk', 'fold')
The draws below stay inside these ranges and needn't reach their ends.
Inputs may be any that keep to these rules, and one draw needn't show every extreme that they name: `genotypes`: dosages are 0, 1 or 2. `trait_order`: a permutation of the 32 traits.
All inputs are finite; a program needn't handle non-finite values.
Results may differ from the reference program's by a relative error of at most 0.00235.
Values may be sent and summed in bfloat16 or wider, within the bound.
No kernel may reach another device: no remote copies, remote signals or barrier semaphores. Data moves between devices by JAX's collectives and lax.ppermute only.
A program may use at most 320 MiB of HBM per device.

```python
import jax
import jax.numpy as jnp
from jax import lax

S_DEV = 8192
B = 512
P_SIZE = 32
R = 2
ITERS = 8
SEG = 32
NB = 16
NVAR = 8192
NSAMP = 131072
Q = 32
N_FOLD = 16


def segment_bits(key, segment, fold_of):
    seg_key = jax.random.fold_in(key, segment)
    permille = jax.random.randint(jax.random.fold_in(seg_key, 0), (), 50, 301)
    fold_total = NSAMP // S_DEV
    allele_freq = permille * (fold_total - 1 + 2 * fold_of) // (2 * (fold_total - 1))
    ancestor = (jax.random.randint(jax.random.fold_in(seg_key, 1), (2, NSAMP), 0, 1000) < allele_freq[None, :]).astype(jnp.int32)
    copied = jax.random.randint(jax.random.fold_in(seg_key, 2), (2, NSAMP, SEG), 0, 1000) < 700
    fresh_bits = (jax.random.randint(jax.random.fold_in(seg_key, 3), (2, NSAMP, SEG), 0, 1000) < allele_freq[None, :, None]).astype(jnp.int32)
    hap_bits = jnp.where(copied, ancestor[:, :, None], fresh_bits)
    return (ancestor, hap_bits, allele_freq)


def draw_genotypes(key, part):
    fold_of = jnp.arange(NSAMP, dtype=jnp.int32) // S_DEV

    def per_segment(segment):
        ancestor, hap_bits, allele_freq = segment_bits(key, segment, fold_of)
        return (hap_bits[0] + hap_bits[1]).astype(jnp.float32).astype(jnp.bfloat16)
    pieces = lax.map(per_segment, jnp.arange(NVAR // SEG, dtype=jnp.int32))
    return jnp.transpose(pieces, (1, 0, 2)).reshape(NSAMP, NVAR)


def draw_phenotypes(key, part):
    fold_of = jnp.arange(NSAMP, dtype=jnp.int32) // S_DEV
    seg_total = NVAR // SEG

    def per_segment(segment):
        ancestor, hap_bits, allele_freq = segment_bits(key, segment, fold_of)
        return (ancestor[0] + ancestor[1]).astype(jnp.float32) - 2.0 * allele_freq.astype(jnp.float32) / 1000.0
    centered = lax.map(per_segment, jnp.arange(seg_total, dtype=jnp.int32))
    effects = jax.random.normal(jax.random.fold_in(key, 1000003), (P_SIZE, seg_total), jnp.float32) * jnp.sqrt(0.5 / (seg_total * 0.3))
    genetic = jnp.dot(effects, centered)
    noise_term = jax.random.normal(jax.random.fold_in(key, 1000004), (P_SIZE, NSAMP), jnp.float32) * 0.7071
    return jnp.clip(genetic + noise_term, -4.0, 4.0).astype(jnp.bfloat16)


def setup_inputs(seed: int = 0) -> dict:
    keys = jax.random.split(jax.random.key(seed), 4)
    genotypes = draw_genotypes(jax.random.fold_in(keys[3], 71), 0)
    phenotypes = draw_phenotypes(jax.random.fold_in(keys[3], 71), 0)
    trait_order = jax.random.permutation(keys[2], P_SIZE).astype(jnp.int32)
    return {"genotypes": genotypes, "phenotypes": phenotypes, "trait_order": trait_order}


LAMBDAS = (0.2, 2.0)
LEVEL_ONE = 0.1
EPSILON = 1e-06

def chebyshev(times_system, target, low_edge, high_edge):
    center = 0.5 * (high_edge + low_edge)
    radius = 0.5 * (high_edge - low_edge)
    sigma_ratio = center / radius
    rho_now = 1.0 / sigma_ratio
    direction = target / center
    solution = jnp.zeros_like(target)
    residual = target
    for iteration in range(ITERS):
        solution = solution + direction
        if iteration + 1 < ITERS:
            residual = residual - times_system(direction)
            rho_next = 1.0 / (2.0 * sigma_ratio - rho_now)
            direction = rho_next * rho_now * direction + 2.0 * rho_next / radius * residual
            rho_now = rho_next
    return solution

def reference(genotypes, phenotypes, trait_order):
    total_rows = S_DEV * N_FOLD
    held_rows = float(total_rows - S_DEV)
    penalty = jnp.array(LAMBDAS, jnp.float32)
    phen = jnp.take(phenotypes, trait_order, axis=0)
    phen_fold = phen.astype(jnp.float32).reshape(P_SIZE, N_FOLD, S_DEV)
    phen_sums = lax.optimization_barrier(jnp.sum(phen_fold, axis=2)).T
    phen_total = lax.optimization_barrier(jnp.sum(phen_sums, axis=0))
    geno = genotypes.reshape(N_FOLD, S_DEV, NB, B)

    def level_zero(block_index):
        block_dose = lax.dynamic_index_in_dim(geno, block_index, 2, False).astype(jnp.float32)
        gram_fold = jnp.einsum('ksi,ksj->kij', block_dose, block_dose)
        col_fold = lax.optimization_barrier(jnp.sum(block_dose, axis=1))
        cross_fold = jnp.einsum('pks,ksi->kpi', phen_fold, block_dose)
        gram_total = lax.optimization_barrier(jnp.sum(gram_fold, axis=0))
        col_total = lax.optimization_barrier(jnp.sum(col_fold, axis=0))
        cross_total = lax.optimization_barrier(jnp.sum(cross_fold, axis=0))
        mean_dose = col_total / total_rows
        inv_scale = 1.0 / jnp.sqrt(jnp.diagonal(gram_total) / total_rows - mean_dose * mean_dose + EPSILON)

        def one_fold(gram_own, col_own, cross_own, phen_own, dose_own):
            gram_out = gram_total - gram_own
            col_out = col_total - col_own
            cross_out = cross_total - cross_own
            phen_out = phen_total - phen_own
            centered = gram_out - col_out[:, None] * mean_dose[None, :] - mean_dose[:, None] * col_out[None, :] + held_rows * mean_dose[:, None] * mean_dose[None, :]
            system = inv_scale[:, None] * centered * inv_scale[None, :] / held_rows
            target = (cross_out - phen_out[:, None] * mean_dose[None, :]) * inv_scale[None, :] / held_rows
            bound = jnp.max(lax.optimization_barrier(jnp.sum(jnp.abs(system), axis=1)))
            low_edge = penalty[:, None, None]
            high_edge = low_edge + bound

            def times_system(direction):
                return jnp.einsum('rpi,ij->rpj', direction, system, precision=lax.Precision.HIGHEST) + low_edge * direction
            stacked = jnp.broadcast_to(target[None], (R,) + target.shape)
            coef = chebyshev(times_system, stacked, low_edge, high_edge)
            scaled = (inv_scale[None, None, :] * coef).astype(jnp.bfloat16)
            scaled_f32 = scaled.astype(jnp.float32)
            product = jnp.einsum('si,rpi->rps', dose_own, scaled_f32, precision=lax.Precision.HIGHEST)
            offset = jnp.einsum('i,rpi->rp', mean_dose, scaled_f32, precision=lax.Precision.HIGHEST)
            return (product - offset[:, :, None]).astype(jnp.bfloat16)
        return jax.vmap(one_fold)(gram_fold, col_fold, cross_fold, phen_sums, block_dose)
    feats = lax.map(level_zero, jnp.arange(NB, dtype=jnp.int32))
    feats = jnp.transpose(feats, (3, 1, 0, 2, 4)).reshape(P_SIZE, N_FOLD, Q, S_DEV)

    def level_one(operands):
        feat_trait, target_trait = operands
        feat_f32 = feat_trait.astype(jnp.float32)
        hgram_fold = jnp.einsum('kqs,kts->kqt', feat_f32, feat_f32)
        hcross_fold = jnp.einsum('kqs,ks->kq', feat_f32, target_trait)
        hgram_total = lax.optimization_barrier(jnp.sum(hgram_fold, axis=0))
        hcross_total = lax.optimization_barrier(jnp.sum(hcross_fold, axis=0))

        def solve_fold(hgram_own, hcross_own, feat_own):
            hgram_out = hgram_total - hgram_own
            hcross_out = hcross_total - hcross_own
            trace_sum = jnp.trace(hgram_out)
            level_system = hgram_out / held_rows + LEVEL_ONE * trace_sum / (held_rows * Q) * jnp.eye(Q, dtype=jnp.float32)
            factor = jnp.linalg.cholesky(level_system)
            weight = jax.scipy.linalg.cho_solve((factor, True), (hcross_out / held_rows)[:, None])[:, 0]
            return jnp.einsum('q,qs->s', weight, feat_own, precision=lax.Precision.HIGHEST)
        return jax.vmap(solve_fold)(hgram_fold, hcross_fold, feat_f32)
    predict = lax.map(level_one, (feats, phen_fold))
    return predict.reshape(P_SIZE, NSAMP)
```

```python
import jax
import jax.numpy as jnp
from jax import lax
from jax.sharding import PartitionSpec as P

B = 512
ITERS = 8


LAMBDAS = (0.2, 2.0)
LEVEL_ONE = 0.1
EPSILON = 1e-06


def chebyshev(times_system, target, low_edge, high_edge):
    center = 0.5 * (high_edge + low_edge)
    radius = 0.5 * (high_edge - low_edge)
    sigma_ratio = center / radius
    rho_now = 1.0 / sigma_ratio
    direction = target / center
    solution = jnp.zeros_like(target)
    residual = target
    for iteration in range(ITERS):
        solution = solution + direction
        if iteration + 1 < ITERS:
            residual = residual - times_system(direction)
            rho_next = 1.0 / (2.0 * sigma_ratio - rho_now)
            direction = rho_next * rho_now * direction + 2.0 * rho_next / radius * residual
            rho_now = rho_next
    return solution


def butterfly_sum(x, axis):
    n = lax.axis_size(axis)
    if n & (n - 1):
        return lax.psum(x, axis)
    step = 1
    while step < n:
        perm = [(i, i ^ step) for i in range(n)]
        x = x + lax.ppermute(x, axis, perm)
        step *= 2
    return x


def per_device(genotypes, phenotypes, trait_order):
    n_fold = lax.axis_size("fold")
    sample_rows = genotypes.shape[0]
    block_count = genotypes.shape[1] // B
    total_rows = sample_rows * n_fold
    held_rows = float(total_rows - sample_rows)
    geno_blocks = genotypes.reshape(sample_rows, block_count, B)
    phen = jnp.take(phenotypes, trait_order, axis=0)
    p_size = phen.shape[0]
    phen_aug = jnp.concatenate([phen, jnp.ones((1, sample_rows), phen.dtype)], axis=0)
    cross_aug = jnp.dot(phen_aug, genotypes, preferred_element_type=jnp.float32)
    phen_local = jnp.sum(phen.astype(jnp.float32), axis=1)
    phen_row = jnp.zeros((1, genotypes.shape[1]), jnp.float32).at[0, :p_size].set(phen_local)
    sums_local = jnp.concatenate([cross_aug, phen_row], axis=0)
    gram_part = jnp.einsum("sbi,sbj->bij", geno_blocks, geno_blocks, preferred_element_type=jnp.float32)
    gram_sum, sums_total = lax.psum((gram_part, sums_local), "fold")
    phen_total = sums_total[p_size + 1, :p_size]
    cross_aug = cross_aug.reshape(p_size + 1, block_count, B)
    cross_aug_total = sums_total[: p_size + 1].reshape(p_size + 1, block_count, B)
    cross_local = jnp.transpose(cross_aug[:p_size], (1, 0, 2))
    col_local = cross_aug[p_size]
    cross_total = jnp.transpose(cross_aug_total[:p_size], (1, 0, 2))
    col_total = cross_aug_total[p_size]
    mean_dose = col_total / total_rows
    eye = jnp.eye(B, dtype=jnp.bool_)
    gram_diag = jnp.sum(jnp.where(eye[None], gram_sum, 0.0), axis=2)
    inv_scale = 1.0 / jnp.sqrt(gram_diag / total_rows - mean_dose * mean_dose + EPSILON)
    gram_out = gram_sum - gram_part
    col_out = col_total - col_local
    cross_out = cross_total - cross_local
    phen_out = phen_total - phen_local
    centered = (
        gram_out
        - col_out[:, :, None] * mean_dose[:, None, :]
        - mean_dose[:, :, None] * col_out[:, None, :]
        + held_rows * mean_dose[:, :, None] * mean_dose[:, None, :]
    )
    system = inv_scale[:, :, None] * centered * inv_scale[:, None, :] / held_rows
    target = (
        (cross_out - phen_out[None, :, None] * mean_dose[:, None, :])
        * inv_scale[:, None, :]
        / held_rows
    )
    bound = jnp.max(jnp.sum(jnp.abs(system), axis=2), axis=1)
    penalty = jnp.array(LAMBDAS, jnp.float32)
    low_edge = jnp.broadcast_to(penalty[None, :, None, None], (block_count, penalty.shape[0], 1, 1))
    high_edge = low_edge + bound[:, None, None, None]

    def times_system(direction):
        return (
            jnp.einsum(
                "brpi,bij->brpj",
                direction,
                system,
                precision=lax.Precision.HIGHEST,
                preferred_element_type=jnp.float32,
            )
            + low_edge * direction
        )

    stacked = jnp.broadcast_to(target[:, None], (block_count, penalty.shape[0]) + target.shape[1:])
    coef = chebyshev(times_system, stacked, low_edge, high_edge)
    scaled = (inv_scale[:, None, None, :] * coef).astype(jnp.bfloat16)
    offset = jnp.einsum(
        "bi,brpi->pbr", mean_dose, scaled.astype(jnp.float32), precision=lax.Precision.HIGHEST
    )
    product = jnp.stack(
        [
            jnp.einsum(
                "si,rpi->prs",
                genotypes[:, b * B:(b + 1) * B],
                scaled[b],
                preferred_element_type=jnp.float32,
            )
            for b in range(block_count)
        ],
        axis=1,
    )
    feature = (product - offset[:, :, :, None]).astype(jnp.bfloat16)
    owned = lax.all_to_all(feature, "blk", split_axis=0, concat_axis=1, tiled=True)
    own_traits = owned.shape[0]
    feature_count = owned.shape[1] * owned.shape[2]
    level_feat = owned.reshape(own_traits, feature_count, sample_rows)
    target_own = lax.dynamic_slice_in_dim(phen, lax.axis_index("blk") * own_traits, own_traits, 0)
    hgram_own = jnp.einsum(
        "pqs,pts->pqt", level_feat, level_feat, preferred_element_type=jnp.float32
    )
    hcross_own = jnp.einsum(
        "pqs,ps->pq", level_feat, target_own, preferred_element_type=jnp.float32
    )
    level_own = jnp.concatenate([hgram_own, hcross_own[:, :, None]], axis=2)
    level_total = butterfly_sum(level_own, "fold")
    hgram_total = level_total[:, :, :feature_count]
    hcross_total = level_total[:, :, feature_count]
    hgram_out = hgram_total - hgram_own
    hcross_out = hcross_total - hcross_own
    trace_sum = jnp.trace(hgram_out, axis1=1, axis2=2)
    level_system = hgram_out / held_rows + (LEVEL_ONE * trace_sum / (held_rows * feature_count))[
        :, None, None
    ] * jnp.eye(feature_count, dtype=jnp.float32)
    factor = jnp.linalg.cholesky(level_system)
    weight = jax.scipy.linalg.cho_solve((factor, True), (hcross_out / held_rows)[:, :, None])[
        :, :, 0
    ]
    return jnp.einsum(
        "pq,pqs->ps", weight, level_feat.astype(jnp.float32), precision=lax.Precision.HIGHEST
    )


def solution(mesh):
    return jax.shard_map(
        per_device,
        mesh=mesh,
        in_specs=(P("fold", "blk"), P(None, "fold"), P()),
        out_specs=P("blk", "fold"),
        check_vma=False,
    )
```

```python
import jax
import jax.numpy as jnp
from jax import lax
from jax.sharding import PartitionSpec as P

B = 512
ITERS = 8


LAMBDAS = (0.2, 2.0)
LEVEL_ONE = 0.1
EPSILON = 1e-06


def chebyshev(times_system, target, low_edge, high_edge):
    center = 0.5 * (high_edge + low_edge)
    radius = 0.5 * (high_edge - low_edge)
    sigma_ratio = center / radius
    rho_now = 1.0 / sigma_ratio
    direction = target / center
    solution = jnp.zeros_like(target)
    residual = target
    for iteration in range(ITERS):
        solution = solution + direction
        if iteration + 1 < ITERS:
            residual = residual - times_system(direction)
            rho_next = 1.0 / (2.0 * sigma_ratio - rho_now)
            direction = rho_next * rho_now * direction + 2.0 * rho_next / radius * residual
            rho_now = rho_next
    return solution


def butterfly_sum(x, axis):
    n = lax.axis_size(axis)
    if n & (n - 1):
        return lax.psum(x, axis)
    step = 1
    while step < n:
        perm = [(i, i ^ step) for i in range(n)]
        x = x + lax.ppermute(x, axis, perm)
        step *= 2
    return x


def per_device(genotypes, phenotypes, trait_order):
    n_fold = lax.axis_size("fold")
    sample_rows = genotypes.shape[0]
    block_count = genotypes.shape[1] // B
    total_rows = sample_rows * n_fold
    held_rows = float(total_rows - sample_rows)
    phen = jnp.take(phenotypes, trait_order, axis=0)
    p_size = phen.shape[0]
    half = B // 2
    rows = lax.broadcasted_iota(jnp.int32, (half, half), 0)
    cols = lax.broadcasted_iota(jnp.int32, (half, half), 1)
    eye_h = rows == cols

    def pack(gram):
        a11, a12, a22 = gram[:half, :half], gram[:half, half:], gram[half:, half:]
        tile = jnp.where(rows > cols, a11, a22)
        diag = jnp.sum(jnp.where(eye_h, a11, 0.0), axis=1)
        return jnp.concatenate([a12, tile, diag[None]], axis=0)

    def unpack(packed):
        a12, tile, diag = packed[:half], packed[half:B], packed[B]
        tile_t = tile.T
        a22 = jnp.where(rows <= cols, tile, tile_t)
        a11 = jnp.where(rows > cols, tile, jnp.where(rows < cols, tile_t, jnp.where(eye_h, diag[:, None], 0.0)))
        top = jnp.concatenate([a11, a12], axis=1)
        bottom = jnp.concatenate([a12.T, a22], axis=1)
        return jnp.concatenate([top, bottom], axis=0)

    gram_parts = []
    packed_sums = []
    for b in range(block_count):
        xb = genotypes[:, b * B:(b + 1) * B]
        gram_b = jnp.einsum("si,sj->ij", xb, xb, preferred_element_type=jnp.float32)
        gram_parts.append(gram_b)
        if b + 1 < block_count:
            packed = pack(gram_b)
            if packed_sums:
                packed = packed.at[0, 0].add(packed_sums[-1][0, 0] * 0.0)
            packed_sums.append(lax.psum(packed, "fold"))
    phen_aug = jnp.concatenate([phen, jnp.ones((1, sample_rows), phen.dtype)], axis=0)
    cross_aug = jnp.dot(phen_aug, genotypes, preferred_element_type=jnp.float32)
    phen_local = jnp.sum(phen.astype(jnp.float32), axis=1)
    phen_row = jnp.zeros((1, genotypes.shape[1]), jnp.float32).at[0, :p_size].set(phen_local)
    sums_local = jnp.concatenate([cross_aug, phen_row], axis=0)
    last_packed = pack(gram_parts[-1])
    if packed_sums:
        last_packed = last_packed.at[0, 0].add(packed_sums[-1][0, 0] * 0.0)
    last_packed, sums_total = lax.psum((last_packed, sums_local), "fold")
    packed_sums.append(last_packed)
    gram_part = jnp.stack(gram_parts)
    gram_sum = jnp.stack([unpack(p) for p in packed_sums])
    phen_total = sums_total[p_size + 1, :p_size]
    cross_aug = cross_aug.reshape(p_size + 1, block_count, B)
    cross_aug_total = sums_total[: p_size + 1].reshape(p_size + 1, block_count, B)
    cross_local = jnp.transpose(cross_aug[:p_size], (1, 0, 2))
    col_local = cross_aug[p_size]
    cross_total = jnp.transpose(cross_aug_total[:p_size], (1, 0, 2))
    col_total = cross_aug_total[p_size]
    mean_dose = col_total / total_rows
    eye = jnp.eye(B, dtype=jnp.bool_)
    gram_diag = jnp.sum(jnp.where(eye[None], gram_sum, 0.0), axis=2)
    inv_scale = 1.0 / jnp.sqrt(gram_diag / total_rows - mean_dose * mean_dose + EPSILON)
    gram_out = gram_sum - gram_part
    col_out = col_total - col_local
    cross_out = cross_total - cross_local
    phen_out = phen_total - phen_local
    centered = (
        gram_out
        - col_out[:, :, None] * mean_dose[:, None, :]
        - mean_dose[:, :, None] * col_out[:, None, :]
        + held_rows * mean_dose[:, :, None] * mean_dose[:, None, :]
    )
    system = inv_scale[:, :, None] * centered * inv_scale[:, None, :] / held_rows
    target = (
        (cross_out - phen_out[None, :, None] * mean_dose[:, None, :])
        * inv_scale[:, None, :]
        / held_rows
    )
    bound = jnp.max(jnp.sum(jnp.abs(system), axis=2), axis=1)
    penalty = jnp.array(LAMBDAS, jnp.float32)
    low_edge = jnp.broadcast_to(penalty[None, :, None, None], (block_count, penalty.shape[0], 1, 1))
    high_edge = low_edge + bound[:, None, None, None]

    def times_system(direction):
        return (
            jnp.einsum(
                "brpi,bij->brpj",
                direction,
                system,
                precision=lax.Precision.HIGHEST,
                preferred_element_type=jnp.float32,
            )
            + low_edge * direction
        )

    stacked = jnp.broadcast_to(target[:, None], (block_count, penalty.shape[0]) + target.shape[1:])
    coef = chebyshev(times_system, stacked, low_edge, high_edge)
    scaled = (inv_scale[:, None, None, :] * coef).astype(jnp.bfloat16)
    offset = jnp.einsum(
        "bi,brpi->pbr", mean_dose, scaled.astype(jnp.float32), precision=lax.Precision.HIGHEST
    )
    product = jnp.stack(
        [
            jnp.einsum(
                "si,rpi->prs",
                genotypes[:, b * B:(b + 1) * B],
                scaled[b],
                preferred_element_type=jnp.float32,
            )
            for b in range(block_count)
        ],
        axis=1,
    )
    feature = (product - offset[:, :, :, None]).astype(jnp.bfloat16)
    owned = lax.all_to_all(feature, "blk", split_axis=0, concat_axis=1, tiled=True)
    own_traits = owned.shape[0]
    feature_count = owned.shape[1] * owned.shape[2]
    level_feat = owned.reshape(own_traits, feature_count, sample_rows)
    target_own = lax.dynamic_slice_in_dim(phen, lax.axis_index("blk") * own_traits, own_traits, 0)
    hgram_own = jnp.einsum(
        "pqs,pts->pqt", level_feat, level_feat, preferred_element_type=jnp.float32
    )
    hcross_own = jnp.einsum(
        "pqs,ps->pq", level_feat, target_own, preferred_element_type=jnp.float32
    )
    level_own = jnp.concatenate([hgram_own, hcross_own[:, :, None]], axis=2)
    level_total = butterfly_sum(level_own, "fold")
    hgram_total = level_total[:, :, :feature_count]
    hcross_total = level_total[:, :, feature_count]
    hgram_out = hgram_total - hgram_own
    hcross_out = hcross_total - hcross_own
    trace_sum = jnp.trace(hgram_out, axis1=1, axis2=2)
    level_system = hgram_out / held_rows + (LEVEL_ONE * trace_sum / (held_rows * feature_count))[
        :, None, None
    ] * jnp.eye(feature_count, dtype=jnp.float32)
    factor = jnp.linalg.cholesky(level_system)
    weight = jax.scipy.linalg.cho_solve((factor, True), (hcross_out / held_rows)[:, :, None])[
        :, :, 0
    ]
    return jnp.einsum(
        "pq,pqs->ps", weight, level_feat.astype(jnp.float32), precision=lax.Precision.HIGHEST
    )


def solution(mesh):
    return jax.shard_map(
        per_device,
        mesh=mesh,
        in_specs=(P("fold", "blk"), P(None, "fold"), P()),
        out_specs=P("blk", "fold"),
        check_vma=False,
    )
```

```python
import jax
import jax.numpy as jnp
from jax import lax
from jax.sharding import PartitionSpec as P

B = 512
ITERS = 8


LAMBDAS = (0.2, 2.0)
LEVEL_ONE = 0.1
EPSILON = 1e-06


def chebyshev(times_system, target, low_edge, high_edge):
    center = 0.5 * (high_edge + low_edge)
    radius = 0.5 * (high_edge - low_edge)
    sigma_ratio = center / radius
    rho_now = 1.0 / sigma_ratio
    direction = target / center
    solution = jnp.zeros_like(target)
    residual = target
    for iteration in range(ITERS):
        solution = solution + direction
        if iteration + 1 < ITERS:
            residual = residual - times_system(direction)
            rho_next = 1.0 / (2.0 * sigma_ratio - rho_now)
            direction = rho_next * rho_now * direction + 2.0 * rho_next / radius * residual
            rho_now = rho_next
    return solution


def butterfly_sum(x, axis):
    n = lax.axis_size(axis)
    if n & (n - 1):
        return lax.psum(x, axis)
    step = 1
    while step < n:
        perm = [(i, i ^ step) for i in range(n)]
        x = x + lax.ppermute(x, axis, perm)
        step *= 2
    return x


def exchange_sum(arrays, axis):
    n = lax.axis_size(axis)
    flat = jnp.concatenate([a.reshape(-1) for a in arrays])
    size = flat.shape[0]
    unit = n * 8 * 128
    flat = jnp.pad(flat, (0, -(-size // unit) * unit - size))
    pieces = lax.all_to_all(flat.reshape(n, -1, 128), axis, 0, 0, tiled=True)
    chunk = jnp.sum(pieces, axis=0)
    whole = lax.all_to_all(jnp.broadcast_to(chunk[None], (n,) + chunk.shape), axis, 0, 0, tiled=True)
    whole = whole.reshape(-1)
    out = []
    offset = 0
    for a in arrays:
        out.append(whole[offset:offset + a.size].reshape(a.shape))
        offset += a.size
    return out


def per_device(genotypes, phenotypes, trait_order):
    n_fold = lax.axis_size("fold")
    sample_rows = genotypes.shape[0]
    block_count = genotypes.shape[1] // B
    total_rows = sample_rows * n_fold
    held_rows = float(total_rows - sample_rows)
    phen = jnp.take(phenotypes, trait_order, axis=0)
    p_size = phen.shape[0]
    half = B // 2
    rows = lax.broadcasted_iota(jnp.int32, (half, half), 0)
    cols = lax.broadcasted_iota(jnp.int32, (half, half), 1)
    eye_h = rows == cols

    def pack(gram):
        a11, a12, a22 = gram[:half, :half], gram[:half, half:], gram[half:, half:]
        tile = jnp.where(rows > cols, a11, a22)
        diag = jnp.sum(jnp.where(eye_h, a11, 0.0), axis=1)
        return jnp.concatenate([a12, tile, diag[None]], axis=0)

    def unpack(packed):
        a12, tile, diag = packed[:half], packed[half:B], packed[B]
        tile_t = tile.T
        a22 = jnp.where(rows <= cols, tile, tile_t)
        a11 = jnp.where(rows > cols, tile, jnp.where(rows < cols, tile_t, jnp.where(eye_h, diag[:, None], 0.0)))
        top = jnp.concatenate([a11, a12], axis=1)
        bottom = jnp.concatenate([a12.T, a22], axis=1)
        return jnp.concatenate([top, bottom], axis=0)

    gram_parts = []
    for b in range(block_count):
        xb = genotypes[:, b * B:(b + 1) * B]
        gram_parts.append(jnp.einsum("si,sj->ij", xb, xb, preferred_element_type=jnp.float32))
    phen_aug = jnp.concatenate([phen, jnp.ones((1, sample_rows), phen.dtype)], axis=0)
    cross_aug = jnp.dot(phen_aug, genotypes, preferred_element_type=jnp.float32)
    phen_local = jnp.sum(phen.astype(jnp.float32), axis=1)
    phen_row = jnp.zeros((1, genotypes.shape[1]), jnp.float32).at[0, :p_size].set(phen_local)
    sums_local = jnp.concatenate([cross_aug, phen_row], axis=0)
    totals = exchange_sum([pack(g) for g in gram_parts] + [sums_local], "fold")
    sums_total = totals[-1]
    gram_part = jnp.stack(gram_parts)
    gram_sum = jnp.stack([unpack(p) for p in totals[:-1]])
    phen_total = sums_total[p_size + 1, :p_size]
    cross_aug = cross_aug.reshape(p_size + 1, block_count, B)
    cross_aug_total = sums_total[: p_size + 1].reshape(p_size + 1, block_count, B)
    cross_local = jnp.transpose(cross_aug[:p_size], (1, 0, 2))
    col_local = cross_aug[p_size]
    cross_total = jnp.transpose(cross_aug_total[:p_size], (1, 0, 2))
    col_total = cross_aug_total[p_size]
    mean_dose = col_total / total_rows
    eye = jnp.eye(B, dtype=jnp.bool_)
    gram_diag = jnp.sum(jnp.where(eye[None], gram_sum, 0.0), axis=2)
    inv_scale = 1.0 / jnp.sqrt(gram_diag / total_rows - mean_dose * mean_dose + EPSILON)
    gram_out = gram_sum - gram_part
    col_out = col_total - col_local
    cross_out = cross_total - cross_local
    phen_out = phen_total - phen_local
    centered = (
        gram_out
        - col_out[:, :, None] * mean_dose[:, None, :]
        - mean_dose[:, :, None] * col_out[:, None, :]
        + held_rows * mean_dose[:, :, None] * mean_dose[:, None, :]
    )
    system = inv_scale[:, :, None] * centered * inv_scale[:, None, :] / held_rows
    target = (
        (cross_out - phen_out[None, :, None] * mean_dose[:, None, :])
        * inv_scale[:, None, :]
        / held_rows
    )
    bound = jnp.max(jnp.sum(jnp.abs(system), axis=2), axis=1)
    penalty = jnp.array(LAMBDAS, jnp.float32)
    low_edge = jnp.broadcast_to(penalty[None, :, None, None], (block_count, penalty.shape[0], 1, 1))
    high_edge = low_edge + bound[:, None, None, None]

    def times_system(direction):
        return (
            jnp.einsum(
                "brpi,bij->brpj",
                direction,
                system,
                precision=lax.Precision.HIGHEST,
                preferred_element_type=jnp.float32,
            )
            + low_edge * direction
        )

    stacked = jnp.broadcast_to(target[:, None], (block_count, penalty.shape[0]) + target.shape[1:])
    coef = chebyshev(times_system, stacked, low_edge, high_edge)
    scaled = (inv_scale[:, None, None, :] * coef).astype(jnp.bfloat16)
    offset = jnp.einsum(
        "bi,brpi->pbr", mean_dose, scaled.astype(jnp.float32), precision=lax.Precision.HIGHEST
    )
    product = jnp.stack(
        [
            jnp.einsum(
                "si,rpi->prs",
                genotypes[:, b * B:(b + 1) * B],
                scaled[b],
                preferred_element_type=jnp.float32,
            )
            for b in range(block_count)
        ],
        axis=1,
    )
    feature = (product - offset[:, :, :, None]).astype(jnp.bfloat16)
    owned = lax.all_to_all(feature, "blk", split_axis=0, concat_axis=1, tiled=True)
    own_traits = owned.shape[0]
    feature_count = owned.shape[1] * owned.shape[2]
    level_feat = owned.reshape(own_traits, feature_count, sample_rows)
    target_own = lax.dynamic_slice_in_dim(phen, lax.axis_index("blk") * own_traits, own_traits, 0)
    hgram_own = jnp.einsum(
        "pqs,pts->pqt", level_feat, level_feat, preferred_element_type=jnp.float32
    )
    hcross_own = jnp.einsum(
        "pqs,ps->pq", level_feat, target_own, preferred_element_type=jnp.float32
    )
    level_own = jnp.concatenate([hgram_own, hcross_own[:, :, None]], axis=2)
    level_total = butterfly_sum(level_own, "fold")
    hgram_total = level_total[:, :, :feature_count]
    hcross_total = level_total[:, :, feature_count]
    hgram_out = hgram_total - hgram_own
    hcross_out = hcross_total - hcross_own
    trace_sum = jnp.trace(hgram_out, axis1=1, axis2=2)
    level_system = hgram_out / held_rows + (LEVEL_ONE * trace_sum / (held_rows * feature_count))[
        :, None, None
    ] * jnp.eye(feature_count, dtype=jnp.float32)
    factor = jnp.linalg.cholesky(level_system)
    weight = jax.scipy.linalg.cho_solve((factor, True), (hcross_out / held_rows)[:, :, None])[
        :, :, 0
    ]
    return jnp.einsum(
        "pq,pqs->ps", weight, level_feat.astype(jnp.float32), precision=lax.Precision.HIGHEST
    )


def solution(mesh):
    return jax.shard_map(
        per_device,
        mesh=mesh,
        in_specs=(P("fold", "blk"), P(None, "fold"), P()),
        out_specs=P("blk", "fold"),
        check_vma=False,
    )
```

```python
import jax
import jax.numpy as jnp
from jax import lax
from jax.sharding import PartitionSpec as P

B = 512
ITERS = 8


LAMBDAS = (0.2, 2.0)
LEVEL_ONE = 0.1
EPSILON = 1e-06


def chebyshev(times_system, target, low_edge, high_edge):
    center = 0.5 * (high_edge + low_edge)
    radius = 0.5 * (high_edge - low_edge)
    sigma_ratio = center / radius
    rho_now = 1.0 / sigma_ratio
    direction = target / center
    solution = jnp.zeros_like(target)
    residual = target
    for iteration in range(ITERS):
        solution = solution + direction
        if iteration + 1 < ITERS:
            residual = residual - times_system(direction)
            rho_next = 1.0 / (2.0 * sigma_ratio - rho_now)
            direction = rho_next * rho_now * direction + 2.0 * rho_next / radius * residual
            rho_now = rho_next
    return solution


def butterfly_sum(x, axis):
    n = lax.axis_size(axis)
    if n & (n - 1):
        return lax.psum(x, axis)
    stride = 1
    while stride < n:
        radix = min(4, n // stride)
        total = x
        for shift in range(1, radix):
            perm = []
            for i in range(n):
                digit = (i // stride) % radix
                perm.append((i, i + ((digit + shift) % radix - digit) * stride))
            total = total + lax.ppermute(x, axis, perm)
        x = total
        stride *= radix
    return x


def exchange_sum(arrays, axis):
    n = lax.axis_size(axis)
    flat = jnp.concatenate([a.reshape(-1) for a in arrays])
    size = flat.shape[0]
    unit = n * 8 * 128
    flat = jnp.pad(flat, (0, -(-size // unit) * unit - size))
    pieces = lax.all_to_all(flat.reshape(n, -1, 128), axis, 0, 0, tiled=True)
    chunk = jnp.sum(pieces, axis=0)
    whole = lax.all_to_all(jnp.broadcast_to(chunk[None], (n,) + chunk.shape), axis, 0, 0, tiled=True)
    whole = whole.reshape(-1)
    out = []
    offset = 0
    for a in arrays:
        out.append(whole[offset:offset + a.size].reshape(a.shape))
        offset += a.size
    return out


def per_device(genotypes, phenotypes, trait_order):
    n_fold = lax.axis_size("fold")
    sample_rows = genotypes.shape[0]
    block_count = genotypes.shape[1] // B
    total_rows = sample_rows * n_fold
    held_rows = float(total_rows - sample_rows)
    phen = jnp.take(phenotypes, trait_order, axis=0)
    p_size = phen.shape[0]
    half = B // 2
    rows = lax.broadcasted_iota(jnp.int32, (half, half), 0)
    cols = lax.broadcasted_iota(jnp.int32, (half, half), 1)
    eye_h = rows == cols

    def pack(gram):
        a11, a12, a22 = gram[:half, :half], gram[:half, half:], gram[half:, half:]
        tile = jnp.where(rows > cols, a11, a22)
        diag = jnp.sum(jnp.where(eye_h, a11, 0.0), axis=1)
        return jnp.concatenate([a12, tile, diag[None]], axis=0)

    def unpack(packed):
        a12, tile, diag = packed[:half], packed[half:B], packed[B]
        tile_t = tile.T
        a22 = jnp.where(rows <= cols, tile, tile_t)
        a11 = jnp.where(rows > cols, tile, jnp.where(rows < cols, tile_t, jnp.where(eye_h, diag[:, None], 0.0)))
        top = jnp.concatenate([a11, a12], axis=1)
        bottom = jnp.concatenate([a12.T, a22], axis=1)
        return jnp.concatenate([top, bottom], axis=0)

    gram_parts = []
    for b in range(block_count):
        xb = genotypes[:, b * B:(b + 1) * B]
        gram_parts.append(jnp.einsum("si,sj->ij", xb, xb, preferred_element_type=jnp.float32))
    phen_aug = jnp.concatenate([phen, jnp.ones((1, sample_rows), phen.dtype)], axis=0)
    cross_aug = jnp.dot(phen_aug, genotypes, preferred_element_type=jnp.float32)
    phen_local = jnp.sum(phen.astype(jnp.float32), axis=1)
    phen_row = jnp.zeros((1, genotypes.shape[1]), jnp.float32).at[0, :p_size].set(phen_local)
    sums_local = jnp.concatenate([cross_aug, phen_row], axis=0)
    totals = exchange_sum([pack(g) for g in gram_parts] + [sums_local], "fold")
    sums_total = totals[-1]
    gram_part = jnp.stack(gram_parts)
    gram_sum = jnp.stack([unpack(p) for p in totals[:-1]])
    phen_total = sums_total[p_size + 1, :p_size]
    cross_aug = cross_aug.reshape(p_size + 1, block_count, B)
    cross_aug_total = sums_total[: p_size + 1].reshape(p_size + 1, block_count, B)
    cross_local = jnp.transpose(cross_aug[:p_size], (1, 0, 2))
    col_local = cross_aug[p_size]
    cross_total = jnp.transpose(cross_aug_total[:p_size], (1, 0, 2))
    col_total = cross_aug_total[p_size]
    mean_dose = col_total / total_rows
    eye = jnp.eye(B, dtype=jnp.bool_)
    gram_diag = jnp.sum(jnp.where(eye[None], gram_sum, 0.0), axis=2)
    inv_scale = 1.0 / jnp.sqrt(gram_diag / total_rows - mean_dose * mean_dose + EPSILON)
    gram_out = gram_sum - gram_part
    col_out = col_total - col_local
    cross_out = cross_total - cross_local
    phen_out = phen_total - phen_local
    centered = (
        gram_out
        - col_out[:, :, None] * mean_dose[:, None, :]
        - mean_dose[:, :, None] * col_out[:, None, :]
        + held_rows * mean_dose[:, :, None] * mean_dose[:, None, :]
    )
    system = inv_scale[:, :, None] * centered * inv_scale[:, None, :] / held_rows
    target = (
        (cross_out - phen_out[None, :, None] * mean_dose[:, None, :])
        * inv_scale[:, None, :]
        / held_rows
    )
    bound = jnp.max(jnp.sum(jnp.abs(system), axis=2), axis=1)
    penalty = jnp.array(LAMBDAS, jnp.float32)
    low_edge = jnp.broadcast_to(penalty[None, :, None, None], (block_count, penalty.shape[0], 1, 1))
    high_edge = low_edge + bound[:, None, None, None]

    def times_system(direction):
        return (
            jnp.einsum(
                "brpi,bij->brpj",
                direction,
                system,
                precision=lax.Precision.HIGHEST,
                preferred_element_type=jnp.float32,
            )
            + low_edge * direction
        )

    stacked = jnp.broadcast_to(target[:, None], (block_count, penalty.shape[0]) + target.shape[1:])
    coef = chebyshev(times_system, stacked, low_edge, high_edge)
    scaled = (inv_scale[:, None, None, :] * coef).astype(jnp.bfloat16)
    offset = jnp.einsum(
        "bi,brpi->pbr", mean_dose, scaled.astype(jnp.float32), precision=lax.Precision.HIGHEST
    )
    product = jnp.stack(
        [
            jnp.einsum(
                "si,rpi->prs",
                genotypes[:, b * B:(b + 1) * B],
                scaled[b],
                preferred_element_type=jnp.float32,
            )
            for b in range(block_count)
        ],
        axis=1,
    )
    feature = (product - offset[:, :, :, None]).astype(jnp.bfloat16)
    owned = lax.all_to_all(feature, "blk", split_axis=0, concat_axis=1, tiled=True)
    own_traits = owned.shape[0]
    feature_count = owned.shape[1] * owned.shape[2]
    level_feat = owned.reshape(own_traits, feature_count, sample_rows)
    target_own = lax.dynamic_slice_in_dim(phen, lax.axis_index("blk") * own_traits, own_traits, 0)
    hgram_own = jnp.einsum(
        "pqs,pts->pqt", level_feat, level_feat, preferred_element_type=jnp.float32
    )
    hcross_own = jnp.einsum(
        "pqs,ps->pq", level_feat, target_own, preferred_element_type=jnp.float32
    )
    level_own = jnp.concatenate([hgram_own, hcross_own[:, :, None]], axis=2)
    level_total = butterfly_sum(level_own, "fold")
    hgram_total = level_total[:, :, :feature_count]
    hcross_total = level_total[:, :, feature_count]
    hgram_out = hgram_total - hgram_own
    hcross_out = hcross_total - hcross_own
    trace_sum = jnp.trace(hgram_out, axis1=1, axis2=2)
    level_system = hgram_out / held_rows + (LEVEL_ONE * trace_sum / (held_rows * feature_count))[
        :, None, None
    ] * jnp.eye(feature_count, dtype=jnp.float32)
    factor = jnp.linalg.cholesky(level_system)
    weight = jax.scipy.linalg.cho_solve((factor, True), (hcross_out / held_rows)[:, :, None])[
        :, :, 0
    ]
    return jnp.einsum(
        "pq,pqs->ps", weight, level_feat.astype(jnp.float32), precision=lax.Precision.HIGHEST
    )


def solution(mesh):
    return jax.shard_map(
        per_device,
        mesh=mesh,
        in_specs=(P("fold", "blk"), P(None, "fold"), P()),
        out_specs=P("blk", "fold"),
        check_vma=False,
    )
```

```python
import jax
import jax.numpy as jnp
from jax import lax
from jax.experimental import pallas as pl
from jax.sharding import PartitionSpec as P

B = 512
ITERS = 8


LAMBDAS = (0.2, 2.0)
LEVEL_ONE = 0.1
EPSILON = 1e-06


def chebyshev(times_system, target, low_edge, high_edge):
    center = 0.5 * (high_edge + low_edge)
    radius = 0.5 * (high_edge - low_edge)
    sigma_ratio = center / radius
    rho_now = 1.0 / sigma_ratio
    direction = target / center
    solution = jnp.zeros_like(target)
    residual = target
    for iteration in range(ITERS):
        solution = solution + direction
        if iteration + 1 < ITERS:
            residual = residual - times_system(direction)
            rho_next = 1.0 / (2.0 * sigma_ratio - rho_now)
            direction = rho_next * rho_now * direction + 2.0 * rho_next / radius * residual
            rho_now = rho_next
    return solution


def _spd_solve_kernel(a_ref, b_ref, w_ref):
    a = a_ref[...]
    b = b_ref[...]
    t, q, _ = a.shape
    rowi = lax.broadcasted_iota(jnp.int32, (t, q, 1), 1)
    coli = lax.broadcasted_iota(jnp.int32, (t, 1, q), 2)
    y = jnp.zeros_like(b)
    columns = []
    for k in range(q):
        s = jnp.sqrt(a[:, k:k + 1, k:k + 1])
        lcol = jnp.where(rowi == k, s, jnp.where(rowi > k, a[:, :, k:k + 1] / s, 0.0))
        lrow = jnp.where(coli == k, s, jnp.where(coli > k, a[:, k:k + 1, :] / s, 0.0))
        a = a - lcol * lrow
        yk = b[:, k:k + 1, :] / s
        b = b - jnp.where(rowi > k, lcol * yk, 0.0)
        y = jnp.where(rowi == k, yk, y)
        columns.append(lcol)
    w = jnp.zeros_like(b)
    for k in reversed(range(q)):
        lcol = columns[k]
        acc = jnp.sum(jnp.where(rowi > k, lcol * w, 0.0), axis=1, keepdims=True)
        w = jnp.where(rowi == k, (y[:, k:k + 1, :] - acc) / lcol[:, k:k + 1, :], w)
    w_ref[...] = w


def spd_solve(a, b):
    return pl.pallas_call(
        _spd_solve_kernel,
        out_shape=jax.ShapeDtypeStruct(b.shape, jnp.float32),
    )(a, b)


def butterfly_sum(x, axis):
    n = lax.axis_size(axis)
    if n & (n - 1):
        return lax.psum(x, axis)
    stride = 1
    while stride < n:
        radix = min(4, n // stride)
        total = x
        for shift in range(1, radix):
            perm = []
            for i in range(n):
                digit = (i // stride) % radix
                perm.append((i, i + ((digit + shift) % radix - digit) * stride))
            total = total + lax.ppermute(x, axis, perm)
        x = total
        stride *= radix
    return x


def exchange_sum(arrays, axis):
    n = lax.axis_size(axis)
    flat = jnp.concatenate([a.reshape(-1) for a in arrays])
    size = flat.shape[0]
    unit = n * 8 * 128
    flat = jnp.pad(flat, (0, -(-size // unit) * unit - size))
    pieces = lax.all_to_all(flat.reshape(n, -1, 128), axis, 0, 0, tiled=True)
    chunk = jnp.sum(pieces, axis=0)
    whole = lax.all_to_all(jnp.broadcast_to(chunk[None], (n,) + chunk.shape), axis, 0, 0, tiled=True)
    whole = whole.reshape(-1)
    out = []
    offset = 0
    for a in arrays:
        out.append(whole[offset:offset + a.size].reshape(a.shape))
        offset += a.size
    return out


def per_device(genotypes, phenotypes, trait_order):
    n_fold = lax.axis_size("fold")
    sample_rows = genotypes.shape[0]
    block_count = genotypes.shape[1] // B
    total_rows = sample_rows * n_fold
    held_rows = float(total_rows - sample_rows)
    phen = jnp.take(phenotypes, trait_order, axis=0)
    p_size = phen.shape[0]
    half = B // 2
    rows = lax.broadcasted_iota(jnp.int32, (half, half), 0)
    cols = lax.broadcasted_iota(jnp.int32, (half, half), 1)
    eye_h = rows == cols

    def pack(gram):
        a11, a12, a22 = gram[:half, :half], gram[:half, half:], gram[half:, half:]
        tile = jnp.where(rows > cols, a11, a22)
        diag = jnp.sum(jnp.where(eye_h, a11, 0.0), axis=1)
        return jnp.concatenate([a12, tile, diag[None]], axis=0)

    def unpack(packed):
        a12, tile, diag = packed[:half], packed[half:B], packed[B]
        tile_t = tile.T
        a22 = jnp.where(rows <= cols, tile, tile_t)
        a11 = jnp.where(rows > cols, tile, jnp.where(rows < cols, tile_t, jnp.where(eye_h, diag[:, None], 0.0)))
        top = jnp.concatenate([a11, a12], axis=1)
        bottom = jnp.concatenate([a12.T, a22], axis=1)
        return jnp.concatenate([top, bottom], axis=0)

    gram_parts = []
    for b in range(block_count):
        xb = genotypes[:, b * B:(b + 1) * B]
        gram_parts.append(jnp.einsum("si,sj->ij", xb, xb, preferred_element_type=jnp.float32))
    phen_aug = jnp.concatenate([phen, jnp.ones((1, sample_rows), phen.dtype)], axis=0)
    cross_aug = jnp.dot(phen_aug, genotypes, preferred_element_type=jnp.float32)
    phen_local = jnp.sum(phen.astype(jnp.float32), axis=1)
    phen_row = jnp.zeros((1, genotypes.shape[1]), jnp.float32).at[0, :p_size].set(phen_local)
    sums_local = jnp.concatenate([cross_aug, phen_row], axis=0)
    totals = exchange_sum([pack(g) for g in gram_parts] + [sums_local], "fold")
    sums_total = totals[-1]
    gram_part = jnp.stack(gram_parts)
    gram_sum = jnp.stack([unpack(p) for p in totals[:-1]])
    phen_total = sums_total[p_size + 1, :p_size]
    cross_aug = cross_aug.reshape(p_size + 1, block_count, B)
    cross_aug_total = sums_total[: p_size + 1].reshape(p_size + 1, block_count, B)
    cross_local = jnp.transpose(cross_aug[:p_size], (1, 0, 2))
    col_local = cross_aug[p_size]
    cross_total = jnp.transpose(cross_aug_total[:p_size], (1, 0, 2))
    col_total = cross_aug_total[p_size]
    mean_dose = col_total / total_rows
    eye = jnp.eye(B, dtype=jnp.bool_)
    gram_diag = jnp.sum(jnp.where(eye[None], gram_sum, 0.0), axis=2)
    inv_scale = 1.0 / jnp.sqrt(gram_diag / total_rows - mean_dose * mean_dose + EPSILON)
    gram_out = gram_sum - gram_part
    col_out = col_total - col_local
    cross_out = cross_total - cross_local
    phen_out = phen_total - phen_local
    centered = (
        gram_out
        - col_out[:, :, None] * mean_dose[:, None, :]
        - mean_dose[:, :, None] * col_out[:, None, :]
        + held_rows * mean_dose[:, :, None] * mean_dose[:, None, :]
    )
    system = inv_scale[:, :, None] * centered * inv_scale[:, None, :] / held_rows
    target = (
        (cross_out - phen_out[None, :, None] * mean_dose[:, None, :])
        * inv_scale[:, None, :]
        / held_rows
    )
    bound = jnp.max(jnp.sum(jnp.abs(system), axis=2), axis=1)
    penalty = jnp.array(LAMBDAS, jnp.float32)
    low_edge = jnp.broadcast_to(penalty[None, :, None, None], (block_count, penalty.shape[0], 1, 1))
    high_edge = low_edge + bound[:, None, None, None]

    def times_system(direction):
        return (
            jnp.einsum(
                "brpi,bij->brpj",
                direction,
                system,
                precision=lax.Precision.HIGHEST,
                preferred_element_type=jnp.float32,
            )
            + low_edge * direction
        )

    stacked = jnp.broadcast_to(target[:, None], (block_count, penalty.shape[0]) + target.shape[1:])
    coef = chebyshev(times_system, stacked, low_edge, high_edge)
    scaled = (inv_scale[:, None, None, :] * coef).astype(jnp.bfloat16)
    offset = jnp.einsum(
        "bi,brpi->pbr", mean_dose, scaled.astype(jnp.float32), precision=lax.Precision.HIGHEST
    )
    product = jnp.stack(
        [
            jnp.einsum(
                "si,rpi->prs",
                genotypes[:, b * B:(b + 1) * B],
                scaled[b],
                preferred_element_type=jnp.float32,
            )
            for b in range(block_count)
        ],
        axis=1,
    )
    feature = (product - offset[:, :, :, None]).astype(jnp.bfloat16)
    owned = lax.all_to_all(feature, "blk", split_axis=0, concat_axis=1, tiled=True)
    own_traits = owned.shape[0]
    feature_count = owned.shape[1] * owned.shape[2]
    level_feat = owned.reshape(own_traits, feature_count, sample_rows)
    target_own = lax.dynamic_slice_in_dim(phen, lax.axis_index("blk") * own_traits, own_traits, 0)
    hgram_own = jnp.einsum(
        "pqs,pts->pqt", level_feat, level_feat, preferred_element_type=jnp.float32
    )
    hcross_own = jnp.einsum(
        "pqs,ps->pq", level_feat, target_own, preferred_element_type=jnp.float32
    )
    level_own = jnp.concatenate([hgram_own, hcross_own[:, :, None]], axis=2)
    level_total = butterfly_sum(level_own, "fold")
    hgram_total = level_total[:, :, :feature_count]
    hcross_total = level_total[:, :, feature_count]
    hgram_out = hgram_total - hgram_own
    hcross_out = hcross_total - hcross_own
    trace_sum = jnp.trace(hgram_out, axis1=1, axis2=2)
    level_system = hgram_out / held_rows + (LEVEL_ONE * trace_sum / (held_rows * feature_count))[
        :, None, None
    ] * jnp.eye(feature_count, dtype=jnp.float32)
    weight = spd_solve(level_system, (hcross_out / held_rows)[:, :, None])[:, :, 0]
    return jnp.einsum(
        "pq,pqs->ps", weight, level_feat.astype(jnp.float32), precision=lax.Precision.HIGHEST
    )


def solution(mesh):
    return jax.shard_map(
        per_device,
        mesh=mesh,
        in_specs=(P("fold", "blk"), P(None, "fold"), P()),
        out_specs=P("blk", "fold"),
        check_vma=False,
    )
```

```python
import jax
import jax.numpy as jnp
from jax import lax
from jax.experimental import pallas as pl
from jax.sharding import PartitionSpec as P

B = 512
ITERS = 8


LAMBDAS = (0.2, 2.0)
LEVEL_ONE = 0.1
EPSILON = 1e-06


def chebyshev(times_system, target, low_edge, high_edge):
    center = 0.5 * (high_edge + low_edge)
    radius = 0.5 * (high_edge - low_edge)
    sigma_ratio = center / radius
    rho_now = 1.0 / sigma_ratio
    direction = target / center
    solution = jnp.zeros_like(target)
    residual = target
    for iteration in range(ITERS):
        solution = solution + direction
        if iteration + 1 < ITERS:
            residual = residual - times_system(direction)
            rho_next = 1.0 / (2.0 * sigma_ratio - rho_now)
            direction = rho_next * rho_now * direction + 2.0 * rho_next / radius * residual
            rho_now = rho_next
    return solution


def _spd_solve_kernel(a_ref, b_ref, w_ref):
    a = a_ref[...]
    b = b_ref[...]
    t, q, _ = a.shape
    rowi = lax.broadcasted_iota(jnp.int32, (t, q, 1), 1)
    coli = lax.broadcasted_iota(jnp.int32, (t, 1, q), 2)
    y = jnp.zeros_like(b)
    columns = []
    for k in range(q):
        s = jnp.sqrt(a[:, k:k + 1, k:k + 1])
        lcol = jnp.where(rowi == k, s, jnp.where(rowi > k, a[:, :, k:k + 1] / s, 0.0))
        lrow = jnp.where(coli == k, s, jnp.where(coli > k, a[:, k:k + 1, :] / s, 0.0))
        a = a - lcol * lrow
        yk = b[:, k:k + 1, :] / s
        b = b - jnp.where(rowi > k, lcol * yk, 0.0)
        y = jnp.where(rowi == k, yk, y)
        columns.append(lcol)
    w = jnp.zeros_like(b)
    for k in reversed(range(q)):
        lcol = columns[k]
        acc = jnp.sum(jnp.where(rowi > k, lcol * w, 0.0), axis=1, keepdims=True)
        w = jnp.where(rowi == k, (y[:, k:k + 1, :] - acc) / lcol[:, k:k + 1, :], w)
    w_ref[...] = w


def spd_solve(a, b):
    return pl.pallas_call(
        _spd_solve_kernel,
        out_shape=jax.ShapeDtypeStruct(b.shape, jnp.float32),
    )(a, b)


def butterfly_sum(x, axis):
    n = lax.axis_size(axis)
    if n & (n - 1):
        return lax.psum(x, axis)
    stride = 1
    while stride < n:
        radix = min(4, n // stride)
        total = x
        for shift in range(1, radix):
            perm = []
            for i in range(n):
                digit = (i // stride) % radix
                perm.append((i, i + ((digit + shift) % radix - digit) * stride))
            total = total + lax.ppermute(x, axis, perm)
        x = total
        stride *= radix
    return x


def exchange_sum(arrays, axis):
    n = lax.axis_size(axis)
    flat = jnp.concatenate([a.reshape(-1) for a in arrays])
    size = flat.shape[0]
    unit = n * 8 * 128
    flat = jnp.pad(flat, (0, -(-size // unit) * unit - size))
    pieces = lax.all_to_all(flat.reshape(n, -1, 128), axis, 0, 0, tiled=True)
    chunk = jnp.sum(pieces, axis=0)
    whole = lax.all_to_all(jnp.broadcast_to(chunk[None], (n,) + chunk.shape), axis, 0, 0, tiled=True)
    whole = whole.reshape(-1)
    out = []
    offset = 0
    for a in arrays:
        out.append(whole[offset:offset + a.size].reshape(a.shape))
        offset += a.size
    return out


def per_device(genotypes, phenotypes, trait_order):
    n_fold = lax.axis_size("fold")
    sample_rows = genotypes.shape[0]
    block_count = genotypes.shape[1] // B
    total_rows = sample_rows * n_fold
    held_rows = float(total_rows - sample_rows)
    phen = jnp.take(phenotypes, trait_order, axis=0)
    p_size = phen.shape[0]
    half = B // 2
    rows = lax.broadcasted_iota(jnp.int32, (half, half), 0)
    cols = lax.broadcasted_iota(jnp.int32, (half, half), 1)
    eye_h = rows == cols

    def pack(gram):
        a11, a12, a22 = gram[:half, :half], gram[:half, half:], gram[half:, half:]
        tile = jnp.where(rows > cols, a11, a22)
        diag = jnp.sum(jnp.where(eye_h, a11, 0.0), axis=1)
        return jnp.concatenate([a12, tile, diag[None]], axis=0)

    def unpack(packed):
        a12, tile, diag = packed[:half], packed[half:B], packed[B]
        tile_t = tile.T
        a22 = jnp.where(rows <= cols, tile, tile_t)
        a11 = jnp.where(rows > cols, tile, jnp.where(rows < cols, tile_t, jnp.where(eye_h, diag[:, None], 0.0)))
        top = jnp.concatenate([a11, a12], axis=1)
        bottom = jnp.concatenate([a12.T, a22], axis=1)
        return jnp.concatenate([top, bottom], axis=0)

    gram_parts = []
    early_totals = []
    for b in range(block_count):
        xb = genotypes[:, b * B:(b + 1) * B]
        gram_parts.append(jnp.einsum("si,sj->ij", xb, xb, preferred_element_type=jnp.float32))
        if b + 1 < block_count:
            early_totals += exchange_sum([pack(gram_parts[-1])], "fold")
    phen_aug = jnp.concatenate([phen, jnp.ones((1, sample_rows), phen.dtype)], axis=0)
    cross_aug = jnp.dot(phen_aug, genotypes, preferred_element_type=jnp.float32)
    phen_local = jnp.sum(phen.astype(jnp.float32), axis=1)
    phen_row = jnp.zeros((1, genotypes.shape[1]), jnp.float32).at[0, :p_size].set(phen_local)
    sums_local = jnp.concatenate([cross_aug, phen_row], axis=0)
    totals = early_totals + exchange_sum([pack(gram_parts[-1]), sums_local], "fold")
    sums_total = totals[-1]
    gram_part = jnp.stack(gram_parts)
    gram_sum = jnp.stack([unpack(p) for p in totals[:-1]])
    phen_total = sums_total[p_size + 1, :p_size]
    cross_aug = cross_aug.reshape(p_size + 1, block_count, B)
    cross_aug_total = sums_total[: p_size + 1].reshape(p_size + 1, block_count, B)
    cross_local = jnp.transpose(cross_aug[:p_size], (1, 0, 2))
    col_local = cross_aug[p_size]
    cross_total = jnp.transpose(cross_aug_total[:p_size], (1, 0, 2))
    col_total = cross_aug_total[p_size]
    mean_dose = col_total / total_rows
    eye = jnp.eye(B, dtype=jnp.bool_)
    gram_diag = jnp.sum(jnp.where(eye[None], gram_sum, 0.0), axis=2)
    inv_scale = 1.0 / jnp.sqrt(gram_diag / total_rows - mean_dose * mean_dose + EPSILON)
    gram_out = gram_sum - gram_part
    col_out = col_total - col_local
    cross_out = cross_total - cross_local
    phen_out = phen_total - phen_local
    centered = (
        gram_out
        - col_out[:, :, None] * mean_dose[:, None, :]
        - mean_dose[:, :, None] * col_out[:, None, :]
        + held_rows * mean_dose[:, :, None] * mean_dose[:, None, :]
    )
    system = inv_scale[:, :, None] * centered * inv_scale[:, None, :] / held_rows
    target = (
        (cross_out - phen_out[None, :, None] * mean_dose[:, None, :])
        * inv_scale[:, None, :]
        / held_rows
    )
    bound = jnp.max(jnp.sum(jnp.abs(system), axis=2), axis=1)
    penalty = jnp.array(LAMBDAS, jnp.float32)
    low_edge = jnp.broadcast_to(penalty[None, :, None, None], (block_count, penalty.shape[0], 1, 1))
    high_edge = low_edge + bound[:, None, None, None]

    def times_system(direction):
        return (
            jnp.einsum(
                "brpi,bij->brpj",
                direction,
                system,
                precision=lax.Precision.HIGHEST,
                preferred_element_type=jnp.float32,
            )
            + low_edge * direction
        )

    stacked = jnp.broadcast_to(target[:, None], (block_count, penalty.shape[0]) + target.shape[1:])
    coef = chebyshev(times_system, stacked, low_edge, high_edge)
    scaled = (inv_scale[:, None, None, :] * coef).astype(jnp.bfloat16)
    offset = jnp.einsum(
        "bi,brpi->pbr", mean_dose, scaled.astype(jnp.float32), precision=lax.Precision.HIGHEST
    )
    product = jnp.stack(
        [
            jnp.einsum(
                "si,rpi->prs",
                genotypes[:, b * B:(b + 1) * B],
                scaled[b],
                preferred_element_type=jnp.float32,
            )
            for b in range(block_count)
        ],
        axis=1,
    )
    feature = (product - offset[:, :, :, None]).astype(jnp.bfloat16)
    owned = lax.all_to_all(feature, "blk", split_axis=0, concat_axis=1, tiled=True)
    own_traits = owned.shape[0]
    feature_count = owned.shape[1] * owned.shape[2]
    level_feat = owned.reshape(own_traits, feature_count, sample_rows)
    target_own = lax.dynamic_slice_in_dim(phen, lax.axis_index("blk") * own_traits, own_traits, 0)
    hgram_own = jnp.einsum(
        "pqs,pts->pqt", level_feat, level_feat, preferred_element_type=jnp.float32
    )
    hcross_own = jnp.einsum(
        "pqs,ps->pq", level_feat, target_own, preferred_element_type=jnp.float32
    )
    level_own = jnp.concatenate([hgram_own, hcross_own[:, :, None]], axis=2)
    level_total = butterfly_sum(level_own, "fold")
    hgram_total = level_total[:, :, :feature_count]
    hcross_total = level_total[:, :, feature_count]
    hgram_out = hgram_total - hgram_own
    hcross_out = hcross_total - hcross_own
    trace_sum = jnp.trace(hgram_out, axis1=1, axis2=2)
    level_system = hgram_out / held_rows + (LEVEL_ONE * trace_sum / (held_rows * feature_count))[
        :, None, None
    ] * jnp.eye(feature_count, dtype=jnp.float32)
    weight = spd_solve(level_system, (hcross_out / held_rows)[:, :, None])[:, :, 0]
    return jnp.einsum(
        "pq,pqs->ps", weight, level_feat.astype(jnp.float32), precision=lax.Precision.HIGHEST
    )


def solution(mesh):
    return jax.shard_map(
        per_device,
        mesh=mesh,
        in_specs=(P("fold", "blk"), P(None, "fold"), P()),
        out_specs=P("blk", "fold"),
        check_vma=False,
    )
```

```python
import jax
import jax.numpy as jnp
from jax import lax
from jax.experimental import pallas as pl
from jax.sharding import PartitionSpec as P

B = 512
ITERS = 8


LAMBDAS = (0.2, 2.0)
LEVEL_ONE = 0.1
EPSILON = 1e-06


def chebyshev(times_system, target, low_edge, high_edge):
    center = 0.5 * (high_edge + low_edge)
    radius = 0.5 * (high_edge - low_edge)
    sigma_ratio = center / radius
    rho_now = 1.0 / sigma_ratio
    direction = target / center
    solution = jnp.zeros_like(target)
    residual = target
    for iteration in range(ITERS):
        solution = solution + direction
        if iteration + 1 < ITERS:
            residual = residual - times_system(direction)
            rho_next = 1.0 / (2.0 * sigma_ratio - rho_now)
            direction = rho_next * rho_now * direction + 2.0 * rho_next / radius * residual
            rho_now = rho_next
    return solution


def _spd_solve_kernel(a_ref, b_ref, w_ref):
    a = a_ref[...]
    b = b_ref[...]
    t, q, _ = a.shape
    rowi = lax.broadcasted_iota(jnp.int32, (t, q, 1), 1)
    coli = lax.broadcasted_iota(jnp.int32, (t, 1, q), 2)
    y = jnp.zeros_like(b)
    columns = []
    for k in range(q):
        s = jnp.sqrt(a[:, k:k + 1, k:k + 1])
        lcol = jnp.where(rowi == k, s, jnp.where(rowi > k, a[:, :, k:k + 1] / s, 0.0))
        lrow = jnp.where(coli == k, s, jnp.where(coli > k, a[:, k:k + 1, :] / s, 0.0))
        a = a - lcol * lrow
        yk = b[:, k:k + 1, :] / s
        b = b - jnp.where(rowi > k, lcol * yk, 0.0)
        y = jnp.where(rowi == k, yk, y)
        columns.append(lcol)
    w = jnp.zeros_like(b)
    for k in reversed(range(q)):
        lcol = columns[k]
        acc = jnp.sum(jnp.where(rowi > k, lcol * w, 0.0), axis=1, keepdims=True)
        w = jnp.where(rowi == k, (y[:, k:k + 1, :] - acc) / lcol[:, k:k + 1, :], w)
    w_ref[...] = w


def spd_solve(a, b):
    return pl.pallas_call(
        _spd_solve_kernel,
        out_shape=jax.ShapeDtypeStruct(b.shape, jnp.float32),
    )(a, b)


def butterfly_sum(x, axis):
    n = lax.axis_size(axis)
    if n & (n - 1):
        return lax.psum(x, axis)
    stride = 1
    while stride < n:
        radix = min(4, n // stride)
        total = x
        for shift in range(1, radix):
            perm = []
            for i in range(n):
                digit = (i // stride) % radix
                perm.append((i, i + ((digit + shift) % radix - digit) * stride))
            total = total + lax.ppermute(x, axis, perm)
        x = total
        stride *= radix
    return x


def exchange_sum(arrays, axis):
    n = lax.axis_size(axis)
    flat = jnp.concatenate([a.reshape(-1) for a in arrays])
    size = flat.shape[0]
    unit = n * 8 * 128
    flat = jnp.pad(flat, (0, -(-size // unit) * unit - size))
    pieces = lax.all_to_all(flat.reshape(n, -1, 128), axis, 0, 0, tiled=True)
    chunk = jnp.sum(pieces, axis=0)
    whole = lax.all_to_all(jnp.broadcast_to(chunk[None], (n,) + chunk.shape), axis, 0, 0, tiled=True)
    whole = whole.reshape(-1)
    out = []
    offset = 0
    for a in arrays:
        out.append(whole[offset:offset + a.size].reshape(a.shape))
        offset += a.size
    return out


def per_device(genotypes, phenotypes, trait_order):
    n_fold = lax.axis_size("fold")
    sample_rows = genotypes.shape[0]
    block_count = genotypes.shape[1] // B
    total_rows = sample_rows * n_fold
    held_rows = float(total_rows - sample_rows)
    phen = jnp.take(phenotypes, trait_order, axis=0)
    p_size = phen.shape[0]
    half = B // 2
    rows = lax.broadcasted_iota(jnp.int32, (half, half), 0)
    cols = lax.broadcasted_iota(jnp.int32, (half, half), 1)
    eye_h = rows == cols

    def pack(gram):
        a11, a12, a22 = gram[:half, :half], gram[:half, half:], gram[half:, half:]
        tile = jnp.where(rows > cols, a11, a22)
        diag = jnp.sum(jnp.where(eye_h, a11, 0.0), axis=1)
        return jnp.concatenate([a12, tile, diag[None]], axis=0)

    def unpack(packed):
        a12, tile, diag = packed[:half], packed[half:B], packed[B]
        tile_t = tile.T
        a22 = jnp.where(rows <= cols, tile, tile_t)
        a11 = jnp.where(rows > cols, tile, jnp.where(rows < cols, tile_t, jnp.where(eye_h, diag[:, None], 0.0)))
        top = jnp.concatenate([a11, a12], axis=1)
        bottom = jnp.concatenate([a12.T, a22], axis=1)
        return jnp.concatenate([top, bottom], axis=0)

    gram_parts = []
    early_totals = []
    for b in range(block_count):
        xb = genotypes[:, b * B:(b + 1) * B]
        gram_parts.append(jnp.einsum("si,sj->ij", xb, xb, preferred_element_type=jnp.float32))
        if b + 1 < block_count:
            early_totals += exchange_sum([pack(gram_parts[-1])], "fold")
    phen_aug = jnp.concatenate([phen, jnp.ones((1, sample_rows), phen.dtype)], axis=0)
    cross_aug = jnp.dot(phen_aug, genotypes, preferred_element_type=jnp.float32)
    phen_local = jnp.sum(phen.astype(jnp.float32), axis=1)
    phen_row = jnp.zeros((1, genotypes.shape[1]), jnp.float32).at[0, :p_size].set(phen_local)
    sums_local = jnp.concatenate([cross_aug, phen_row], axis=0)
    totals = early_totals + exchange_sum([pack(gram_parts[-1]), sums_local], "fold")
    sums_total = totals[-1]
    gram_part = jnp.stack(gram_parts)
    gram_sum = jnp.stack([unpack(p) for p in totals[:-1]])
    phen_total = sums_total[p_size + 1, :p_size]
    cross_aug = cross_aug.reshape(p_size + 1, block_count, B)
    cross_aug_total = sums_total[: p_size + 1].reshape(p_size + 1, block_count, B)
    cross_local = jnp.transpose(cross_aug[:p_size], (1, 0, 2))
    col_local = cross_aug[p_size]
    cross_total = jnp.transpose(cross_aug_total[:p_size], (1, 0, 2))
    col_total = cross_aug_total[p_size]
    mean_dose = col_total / total_rows
    eye = jnp.eye(B, dtype=jnp.bool_)
    gram_diag = jnp.sum(jnp.where(eye[None], gram_sum, 0.0), axis=2)
    inv_scale = 1.0 / jnp.sqrt(gram_diag / total_rows - mean_dose * mean_dose + EPSILON)
    gram_out = gram_sum - gram_part
    col_out = col_total - col_local
    cross_out = cross_total - cross_local
    phen_out = phen_total - phen_local
    centered = (
        gram_out
        - col_out[:, :, None] * mean_dose[:, None, :]
        - mean_dose[:, :, None] * col_out[:, None, :]
        + held_rows * mean_dose[:, :, None] * mean_dose[:, None, :]
    )
    system = inv_scale[:, :, None] * centered * inv_scale[:, None, :] / held_rows
    target = (
        (cross_out - phen_out[None, :, None] * mean_dose[:, None, :])
        * inv_scale[:, None, :]
        / held_rows
    )
    bound = jnp.max(jnp.sum(jnp.abs(system), axis=2), axis=1)
    penalty = jnp.array(LAMBDAS, jnp.float32)
    low_edge = jnp.broadcast_to(penalty[None, :, None, None], (block_count, penalty.shape[0], 1, 1))
    high_edge = low_edge + bound[:, None, None, None]

    def times_system(direction):
        return (
            jnp.einsum(
                "brpi,bij->brpj",
                direction,
                system,
                precision=lax.Precision.HIGHEST,
                preferred_element_type=jnp.float32,
            )
            + low_edge * direction
        )

    stacked = jnp.broadcast_to(target[:, None], (block_count, penalty.shape[0]) + target.shape[1:])
    coef = chebyshev(times_system, stacked, low_edge, high_edge)
    scaled = (inv_scale[:, None, None, :] * coef).astype(jnp.bfloat16)
    offset = jnp.einsum(
        "bi,brpi->pbr", mean_dose, scaled.astype(jnp.float32), precision=lax.Precision.HIGHEST
    )
    halves = 2
    part_rows = sample_rows // halves
    blk_index = lax.axis_index("blk")
    level_parts = []
    hgram_own = 0.0
    hcross_own = 0.0
    for h in range(halves):
        rows_h = slice(h * part_rows, (h + 1) * part_rows)
        product = jnp.stack(
            [
                jnp.einsum(
                    "si,rpi->prs",
                    genotypes[rows_h, b * B:(b + 1) * B],
                    scaled[b],
                    preferred_element_type=jnp.float32,
                )
                for b in range(block_count)
            ],
            axis=1,
        )
        feature = (product - offset[:, :, :, None]).astype(jnp.bfloat16)
        owned = lax.all_to_all(feature, "blk", split_axis=0, concat_axis=1, tiled=True)
        own_traits = owned.shape[0]
        feature_count = owned.shape[1] * owned.shape[2]
        level_feat = owned.reshape(own_traits, feature_count, part_rows)
        target_own = lax.dynamic_slice_in_dim(phen[:, rows_h], blk_index * own_traits, own_traits, 0)
        hgram_own = hgram_own + jnp.einsum(
            "pqs,pts->pqt", level_feat, level_feat, preferred_element_type=jnp.float32
        )
        hcross_own = hcross_own + jnp.einsum(
            "pqs,ps->pq", level_feat, target_own, preferred_element_type=jnp.float32
        )
        level_parts.append(level_feat)
    level_own = jnp.concatenate([hgram_own, hcross_own[:, :, None]], axis=2)
    level_total = butterfly_sum(level_own, "fold")
    hgram_total = level_total[:, :, :feature_count]
    hcross_total = level_total[:, :, feature_count]
    hgram_out = hgram_total - hgram_own
    hcross_out = hcross_total - hcross_own
    trace_sum = jnp.trace(hgram_out, axis1=1, axis2=2)
    level_system = hgram_out / held_rows + (LEVEL_ONE * trace_sum / (held_rows * feature_count))[
        :, None, None
    ] * jnp.eye(feature_count, dtype=jnp.float32)
    weight = spd_solve(level_system, (hcross_out / held_rows)[:, :, None])[:, :, 0]
    return jnp.concatenate(
        [
            jnp.einsum("pq,pqs->ps", weight, f.astype(jnp.float32), precision=lax.Precision.HIGHEST)
            for f in level_parts
        ],
        axis=1,
    )


def solution(mesh):
    return jax.shard_map(
        per_device,
        mesh=mesh,
        in_specs=(P("fold", "blk"), P(None, "fold"), P()),
        out_specs=P("blk", "fold"),
        check_vma=False,
    )
```

```python
import jax
import jax.numpy as jnp
from jax import lax
from jax.experimental import pallas as pl
from jax.sharding import PartitionSpec as P

B = 512
ITERS = 8


LAMBDAS = (0.2, 2.0)
LEVEL_ONE = 0.1
EPSILON = 1e-06


def chebyshev(times_system, target, low_edge, high_edge):
    center = 0.5 * (high_edge + low_edge)
    radius = 0.5 * (high_edge - low_edge)
    sigma_ratio = center / radius
    rho_now = 1.0 / sigma_ratio
    direction = target / center
    solution = jnp.zeros_like(target)
    residual = target
    for iteration in range(ITERS):
        solution = solution + direction
        if iteration + 1 < ITERS:
            residual = residual - times_system(direction)
            rho_next = 1.0 / (2.0 * sigma_ratio - rho_now)
            direction = rho_next * rho_now * direction + 2.0 * rho_next / radius * residual
            rho_now = rho_next
    return solution


def _spd_solve_kernel(a_ref, b_ref, w_ref):
    a = a_ref[...]
    b = b_ref[...]
    t, q, _ = a.shape
    rowi = lax.broadcasted_iota(jnp.int32, (t, q, 1), 1)
    coli = lax.broadcasted_iota(jnp.int32, (t, 1, q), 2)
    y = jnp.zeros_like(b)
    columns = []
    for k in range(q):
        s = jnp.sqrt(a[:, k:k + 1, k:k + 1])
        lcol = jnp.where(rowi == k, s, jnp.where(rowi > k, a[:, :, k:k + 1] / s, 0.0))
        lrow = jnp.where(coli == k, s, jnp.where(coli > k, a[:, k:k + 1, :] / s, 0.0))
        a = a - lcol * lrow
        yk = b[:, k:k + 1, :] / s
        b = b - jnp.where(rowi > k, lcol * yk, 0.0)
        y = jnp.where(rowi == k, yk, y)
        columns.append(lcol)
    w = jnp.zeros_like(b)
    for k in reversed(range(q)):
        lcol = columns[k]
        acc = jnp.sum(jnp.where(rowi > k, lcol * w, 0.0), axis=1, keepdims=True)
        w = jnp.where(rowi == k, (y[:, k:k + 1, :] - acc) / lcol[:, k:k + 1, :], w)
    w_ref[...] = w


def spd_solve(a, b):
    return pl.pallas_call(
        _spd_solve_kernel,
        out_shape=jax.ShapeDtypeStruct(b.shape, jnp.float32),
    )(a, b)


def butterfly_sum(x, axis):
    n = lax.axis_size(axis)
    if n & (n - 1):
        return lax.psum(x, axis)
    stride = 1
    while stride < n:
        radix = min(4, n // stride)
        total = x
        for shift in range(1, radix):
            perm = []
            for i in range(n):
                digit = (i // stride) % radix
                perm.append((i, i + ((digit + shift) % radix - digit) * stride))
            total = total + lax.ppermute(x, axis, perm)
        x = total
        stride *= radix
    return x


def scatter_sum(arrays, axis, wire):
    n = lax.axis_size(axis)
    flat = jnp.concatenate([a.reshape(-1) for a in arrays])
    size = flat.shape[0]
    unit = n * 16 * 128
    flat = jnp.pad(flat, (0, -(-size // unit) * unit - size))
    pieces = lax.all_to_all(flat.astype(wire).reshape(n, -1, 128), axis, 0, 0, tiled=True)
    acc = jnp.int32 if jnp.issubdtype(wire, jnp.integer) else jnp.float32
    return jnp.sum(pieces.astype(acc), axis=0).astype(jnp.float32), arrays


def gather_split(parts, axis):
    n = lax.axis_size(axis)
    joined = jnp.concatenate([c for c, _ in parts], axis=0)
    whole = lax.all_to_all(jnp.broadcast_to(joined[None], (n,) + joined.shape), axis, 0, 0, tiled=True)
    out = []
    start = 0
    for chunk, arrays in parts:
        flat = whole[:, start:start + chunk.shape[0]].reshape(-1)
        start += chunk.shape[0]
        offset = 0
        for a in arrays:
            out.append(flat[offset:offset + a.size].reshape(a.shape))
            offset += a.size
    return out


def per_device(genotypes, phenotypes, trait_order):
    n_fold = lax.axis_size("fold")
    sample_rows = genotypes.shape[0]
    block_count = genotypes.shape[1] // B
    total_rows = sample_rows * n_fold
    held_rows = float(total_rows - sample_rows)
    phen = jnp.take(phenotypes, trait_order, axis=0)
    p_size = phen.shape[0]
    half = B // 2
    rows = lax.broadcasted_iota(jnp.int32, (half, half), 0)
    cols = lax.broadcasted_iota(jnp.int32, (half, half), 1)
    eye_h = rows == cols

    def pack(gram):
        a11, a12, a22 = gram[:half, :half], gram[:half, half:], gram[half:, half:]
        tile = jnp.where(rows > cols, a11, a22)
        diag = jnp.sum(jnp.where(eye_h, a11, 0.0), axis=1)
        return jnp.concatenate([a12, tile, diag[None]], axis=0)

    def unpack(packed):
        a12, tile, diag = packed[:half], packed[half:B], packed[B]
        tile_t = tile.T
        a22 = jnp.where(rows <= cols, tile, tile_t)
        a11 = jnp.where(rows > cols, tile, jnp.where(rows < cols, tile_t, jnp.where(eye_h, diag[:, None], 0.0)))
        top = jnp.concatenate([a11, a12], axis=1)
        bottom = jnp.concatenate([a12.T, a22], axis=1)
        return jnp.concatenate([top, bottom], axis=0)

    gram_parts = []
    early_totals = []
    gram_wire = jnp.uint16 if 4 * sample_rows <= 65535 else jnp.float32
    for b in range(block_count):
        xb = genotypes[:, b * B:(b + 1) * B]
        gram_parts.append(jnp.einsum("si,sj->ij", xb, xb, preferred_element_type=jnp.float32))
        if b + 1 < block_count:
            early_totals += gather_split([scatter_sum([pack(gram_parts[-1])], "fold", gram_wire)], "fold")
    phen_aug = jnp.concatenate([phen, jnp.ones((1, sample_rows), phen.dtype)], axis=0)
    cross_aug = jnp.dot(phen_aug, genotypes, preferred_element_type=jnp.float32)
    phen_local = jnp.sum(phen.astype(jnp.float32), axis=1)
    phen_row = jnp.zeros((1, genotypes.shape[1]), jnp.float32).at[0, :p_size].set(phen_local)
    sums_local = jnp.concatenate([cross_aug, phen_row], axis=0)
    totals = early_totals + gather_split(
        [
            scatter_sum([pack(gram_parts[-1])], "fold", gram_wire),
            scatter_sum([sums_local], "fold", jnp.float32),
        ],
        "fold",
    )
    sums_total = totals[-1]
    gram_part = jnp.stack(gram_parts)
    gram_sum = jnp.stack([unpack(p) for p in totals[:-1]])
    phen_total = sums_total[p_size + 1, :p_size]
    cross_aug = cross_aug.reshape(p_size + 1, block_count, B)
    cross_aug_total = sums_total[: p_size + 1].reshape(p_size + 1, block_count, B)
    cross_local = jnp.transpose(cross_aug[:p_size], (1, 0, 2))
    col_local = cross_aug[p_size]
    cross_total = jnp.transpose(cross_aug_total[:p_size], (1, 0, 2))
    col_total = cross_aug_total[p_size]
    mean_dose = col_total / total_rows
    eye = jnp.eye(B, dtype=jnp.bool_)
    gram_diag = jnp.sum(jnp.where(eye[None], gram_sum, 0.0), axis=2)
    inv_scale = 1.0 / jnp.sqrt(gram_diag / total_rows - mean_dose * mean_dose + EPSILON)
    gram_out = gram_sum - gram_part
    col_out = col_total - col_local
    cross_out = cross_total - cross_local
    phen_out = phen_total - phen_local
    centered = (
        gram_out
        - col_out[:, :, None] * mean_dose[:, None, :]
        - mean_dose[:, :, None] * col_out[:, None, :]
        + held_rows * mean_dose[:, :, None] * mean_dose[:, None, :]
    )
    system = inv_scale[:, :, None] * centered * inv_scale[:, None, :] / held_rows
    target = (
        (cross_out - phen_out[None, :, None] * mean_dose[:, None, :])
        * inv_scale[:, None, :]
        / held_rows
    )
    bound = jnp.max(jnp.sum(jnp.abs(system), axis=2), axis=1)
    penalty = jnp.array(LAMBDAS, jnp.float32)
    low_edge = jnp.broadcast_to(penalty[None, :, None, None], (block_count, penalty.shape[0], 1, 1))
    high_edge = low_edge + bound[:, None, None, None]

    def times_system(direction):
        return (
            jnp.einsum(
                "brpi,bij->brpj",
                direction,
                system,
                precision=lax.Precision.HIGHEST,
                preferred_element_type=jnp.float32,
            )
            + low_edge * direction
        )

    stacked = jnp.broadcast_to(target[:, None], (block_count, penalty.shape[0]) + target.shape[1:])
    coef = chebyshev(times_system, stacked, low_edge, high_edge)
    scaled = (inv_scale[:, None, None, :] * coef).astype(jnp.bfloat16)
    offset = jnp.einsum(
        "bi,brpi->pbr", mean_dose, scaled.astype(jnp.float32), precision=lax.Precision.HIGHEST
    )
    halves = 2
    part_rows = sample_rows // halves
    blk_index = lax.axis_index("blk")
    level_parts = []
    hgram_own = 0.0
    hcross_own = 0.0
    for h in range(halves):
        rows_h = slice(h * part_rows, (h + 1) * part_rows)
        product = jnp.stack(
            [
                jnp.einsum(
                    "si,rpi->prs",
                    genotypes[rows_h, b * B:(b + 1) * B],
                    scaled[b],
                    preferred_element_type=jnp.float32,
                )
                for b in range(block_count)
            ],
            axis=1,
        )
        feature = (product - offset[:, :, :, None]).astype(jnp.bfloat16)
        owned = lax.all_to_all(feature, "blk", split_axis=0, concat_axis=1, tiled=True)
        own_traits = owned.shape[0]
        feature_count = owned.shape[1] * owned.shape[2]
        level_feat = owned.reshape(own_traits, feature_count, part_rows)
        target_own = lax.dynamic_slice_in_dim(phen[:, rows_h], blk_index * own_traits, own_traits, 0)
        hgram_own = hgram_own + jnp.einsum(
            "pqs,pts->pqt", level_feat, level_feat, preferred_element_type=jnp.float32
        )
        hcross_own = hcross_own + jnp.einsum(
            "pqs,ps->pq", level_feat, target_own, preferred_element_type=jnp.float32
        )
        level_parts.append(level_feat)
    level_own = jnp.concatenate([hgram_own, hcross_own[:, :, None]], axis=2)
    level_total = butterfly_sum(level_own, "fold")
    hgram_total = level_total[:, :, :feature_count]
    hcross_total = level_total[:, :, feature_count]
    hgram_out = hgram_total - hgram_own
    hcross_out = hcross_total - hcross_own
    trace_sum = jnp.trace(hgram_out, axis1=1, axis2=2)
    level_system = hgram_out / held_rows + (LEVEL_ONE * trace_sum / (held_rows * feature_count))[
        :, None, None
    ] * jnp.eye(feature_count, dtype=jnp.float32)
    weight = spd_solve(level_system, (hcross_out / held_rows)[:, :, None])[:, :, 0]
    return jnp.concatenate(
        [
            jnp.einsum("pq,pqs->ps", weight, f.astype(jnp.float32), precision=lax.Precision.HIGHEST)
            for f in level_parts
        ],
        axis=1,
    )


def solution(mesh):
    return jax.shard_map(
        per_device,
        mesh=mesh,
        in_specs=(P("fold", "blk"), P(None, "fold"), P()),
        out_specs=P("blk", "fold"),
        check_vma=False,
    )
```

```python
import jax
import jax.numpy as jnp
from jax import lax
from jax.experimental import pallas as pl
from jax.sharding import PartitionSpec as P

B = 512
ITERS = 8


LAMBDAS = (0.2, 2.0)
LEVEL_ONE = 0.1
EPSILON = 1e-06


def chebyshev(times_system, target, low_edge, high_edge):
    center = 0.5 * (high_edge + low_edge)
    radius = 0.5 * (high_edge - low_edge)
    sigma_ratio = center / radius
    rho_now = 1.0 / sigma_ratio
    direction = target / center
    solution = jnp.zeros_like(target)
    residual = target
    for iteration in range(ITERS):
        solution = solution + direction
        if iteration + 1 < ITERS:
            residual = residual - times_system(direction)
            rho_next = 1.0 / (2.0 * sigma_ratio - rho_now)
            direction = rho_next * rho_now * direction + 2.0 * rho_next / radius * residual
            rho_now = rho_next
    return solution


def _spd_solve_kernel(a_ref, b_ref, w_ref):
    a = a_ref[...]
    b = b_ref[...]
    t, q, _ = a.shape
    rowi = lax.broadcasted_iota(jnp.int32, (t, q, 1), 1)
    coli = lax.broadcasted_iota(jnp.int32, (t, 1, q), 2)
    y = jnp.zeros_like(b)
    columns = []
    for k in range(q):
        s = jnp.sqrt(a[:, k:k + 1, k:k + 1])
        lcol = jnp.where(rowi == k, s, jnp.where(rowi > k, a[:, :, k:k + 1] / s, 0.0))
        lrow = jnp.where(coli == k, s, jnp.where(coli > k, a[:, k:k + 1, :] / s, 0.0))
        a = a - lcol * lrow
        yk = b[:, k:k + 1, :] / s
        b = b - jnp.where(rowi > k, lcol * yk, 0.0)
        y = jnp.where(rowi == k, yk, y)
        columns.append(lcol)
    w = jnp.zeros_like(b)
    for k in reversed(range(q)):
        lcol = columns[k]
        acc = jnp.sum(jnp.where(rowi > k, lcol * w, 0.0), axis=1, keepdims=True)
        w = jnp.where(rowi == k, (y[:, k:k + 1, :] - acc) / lcol[:, k:k + 1, :], w)
    w_ref[...] = w


def spd_solve(a, b):
    return pl.pallas_call(
        _spd_solve_kernel,
        out_shape=jax.ShapeDtypeStruct(b.shape, jnp.float32),
    )(a, b)


def butterfly_sum(x, axis):
    n = lax.axis_size(axis)
    if n & (n - 1):
        return lax.psum(x, axis)
    stride = 1
    while stride < n:
        radix = min(4, n // stride)
        total = x
        for shift in range(1, radix):
            perm = []
            for i in range(n):
                digit = (i // stride) % radix
                perm.append((i, i + ((digit + shift) % radix - digit) * stride))
            total = total + lax.ppermute(x, axis, perm)
        x = total
        stride *= radix
    return x


def exchange_sum(arrays, axis):
    n = lax.axis_size(axis)
    flat = jnp.concatenate([a.reshape(-1) for a in arrays])
    size = flat.shape[0]
    unit = n * 8 * 128
    flat = jnp.pad(flat, (0, -(-size // unit) * unit - size))
    pieces = lax.all_to_all(flat.reshape(n, -1, 128), axis, 0, 0, tiled=True)
    chunk = jnp.sum(pieces, axis=0)
    whole = lax.all_to_all(jnp.broadcast_to(chunk[None], (n,) + chunk.shape), axis, 0, 0, tiled=True)
    whole = whole.reshape(-1)
    out = []
    offset = 0
    for a in arrays:
        out.append(whole[offset:offset + a.size].reshape(a.shape))
        offset += a.size
    return out


def per_device(genotypes, phenotypes, trait_order):
    n_fold = lax.axis_size("fold")
    sample_rows = genotypes.shape[0]
    block_count = genotypes.shape[1] // B
    total_rows = sample_rows * n_fold
    held_rows = float(total_rows - sample_rows)
    phen = jnp.take(phenotypes, trait_order, axis=0)
    p_size = phen.shape[0]
    half = B // 2
    rows = lax.broadcasted_iota(jnp.int32, (half, half), 0)
    cols = lax.broadcasted_iota(jnp.int32, (half, half), 1)
    eye_h = rows == cols

    def pack(gram):
        a11, a12, a22 = gram[:half, :half], gram[:half, half:], gram[half:, half:]
        tile = jnp.where(rows > cols, a11, a22)
        diag = jnp.sum(jnp.where(eye_h, a11, 0.0), axis=1)
        return jnp.concatenate([a12, tile, diag[None]], axis=0)

    def unpack(packed):
        a12, tile, diag = packed[:half], packed[half:B], packed[B]
        tile_t = tile.T
        a22 = jnp.where(rows <= cols, tile, tile_t)
        a11 = jnp.where(rows > cols, tile, jnp.where(rows < cols, tile_t, jnp.where(eye_h, diag[:, None], 0.0)))
        top = jnp.concatenate([a11, a12], axis=1)
        bottom = jnp.concatenate([a12.T, a22], axis=1)
        return jnp.concatenate([top, bottom], axis=0)

    gram_parts = []
    early_totals = []
    for b in range(block_count):
        xb = genotypes[:, b * B:(b + 1) * B]
        gram_parts.append(jnp.einsum("si,sj->ij", xb, xb, preferred_element_type=jnp.float32))
        if b + 1 < block_count:
            early_totals += exchange_sum([pack(gram_parts[-1])], "fold")
    phen_aug = jnp.concatenate([phen, jnp.ones((1, sample_rows), phen.dtype)], axis=0)
    cross_aug = jnp.dot(phen_aug, genotypes, preferred_element_type=jnp.float32)
    phen_local = jnp.sum(phen.astype(jnp.float32), axis=1)
    phen_row = jnp.zeros((1, genotypes.shape[1]), jnp.float32).at[0, :p_size].set(phen_local)
    sums_local = jnp.concatenate([cross_aug, phen_row], axis=0)
    totals = early_totals + exchange_sum([pack(gram_parts[-1]), sums_local], "fold")
    sums_total = totals[-1]
    gram_part = jnp.stack(gram_parts)
    gram_sum = jnp.stack([unpack(p) for p in totals[:-1]])
    phen_total = sums_total[p_size + 1, :p_size]
    cross_aug = cross_aug.reshape(p_size + 1, block_count, B)
    cross_aug_total = sums_total[: p_size + 1].reshape(p_size + 1, block_count, B)
    cross_local = jnp.transpose(cross_aug[:p_size], (1, 0, 2))
    col_local = cross_aug[p_size]
    cross_total = jnp.transpose(cross_aug_total[:p_size], (1, 0, 2))
    col_total = cross_aug_total[p_size]
    mean_dose = col_total / total_rows
    eye = jnp.eye(B, dtype=jnp.bool_)
    gram_diag = jnp.sum(jnp.where(eye[None], gram_sum, 0.0), axis=2)
    inv_scale = 1.0 / jnp.sqrt(gram_diag / total_rows - mean_dose * mean_dose + EPSILON)
    gram_out = gram_sum - gram_part
    col_out = col_total - col_local
    cross_out = cross_total - cross_local
    phen_out = phen_total - phen_local
    centered = (
        gram_out
        - col_out[:, :, None] * mean_dose[:, None, :]
        - mean_dose[:, :, None] * col_out[:, None, :]
        + held_rows * mean_dose[:, :, None] * mean_dose[:, None, :]
    )
    system = inv_scale[:, :, None] * centered * inv_scale[:, None, :] / held_rows
    target = (
        (cross_out - phen_out[None, :, None] * mean_dose[:, None, :])
        * inv_scale[:, None, :]
        / held_rows
    )
    bound = jnp.max(jnp.sum(jnp.abs(system), axis=2), axis=1)
    penalty = jnp.array(LAMBDAS, jnp.float32)
    low_edge = jnp.broadcast_to(penalty[None, :, None, None], (block_count, penalty.shape[0], 1, 1))
    high_edge = low_edge + bound[:, None, None, None]

    def times_system(direction):
        return (
            jnp.einsum(
                "brpi,bij->brpj",
                direction,
                system,
                precision=lax.Precision.HIGH,
                preferred_element_type=jnp.float32,
            )
            + low_edge * direction
        )

    stacked = jnp.broadcast_to(target[:, None], (block_count, penalty.shape[0]) + target.shape[1:])
    coef = chebyshev(times_system, stacked, low_edge, high_edge)
    scaled = (inv_scale[:, None, None, :] * coef).astype(jnp.bfloat16)
    offset = jnp.einsum(
        "bi,brpi->pbr", mean_dose, scaled.astype(jnp.float32), precision=lax.Precision.HIGHEST
    )
    halves = 2
    part_rows = sample_rows // halves
    blk_index = lax.axis_index("blk")
    level_parts = []
    hgram_own = 0.0
    hcross_own = 0.0
    for h in range(halves):
        rows_h = slice(h * part_rows, (h + 1) * part_rows)
        product = jnp.stack(
            [
                jnp.einsum(
                    "si,rpi->prs",
                    genotypes[rows_h, b * B:(b + 1) * B],
                    scaled[b],
                    preferred_element_type=jnp.float32,
                )
                for b in range(block_count)
            ],
            axis=1,
        )
        feature = (product - offset[:, :, :, None]).astype(jnp.bfloat16)
        owned = lax.all_to_all(feature, "blk", split_axis=0, concat_axis=1, tiled=True)
        own_traits = owned.shape[0]
        feature_count = owned.shape[1] * owned.shape[2]
        level_feat = owned.reshape(own_traits, feature_count, part_rows)
        target_own = lax.dynamic_slice_in_dim(phen[:, rows_h], blk_index * own_traits, own_traits, 0)
        hgram_own = hgram_own + jnp.einsum(
            "pqs,pts->pqt", level_feat, level_feat, preferred_element_type=jnp.float32
        )
        hcross_own = hcross_own + jnp.einsum(
            "pqs,ps->pq", level_feat, target_own, preferred_element_type=jnp.float32
        )
        level_parts.append(level_feat)
    level_own = jnp.concatenate([hgram_own, hcross_own[:, :, None]], axis=2)
    level_total = butterfly_sum(level_own, "fold")
    hgram_total = level_total[:, :, :feature_count]
    hcross_total = level_total[:, :, feature_count]
    hgram_out = hgram_total - hgram_own
    hcross_out = hcross_total - hcross_own
    trace_sum = jnp.trace(hgram_out, axis1=1, axis2=2)
    level_system = hgram_out / held_rows + (LEVEL_ONE * trace_sum / (held_rows * feature_count))[
        :, None, None
    ] * jnp.eye(feature_count, dtype=jnp.float32)
    weight = spd_solve(level_system, (hcross_out / held_rows)[:, :, None])[:, :, 0]
    return jnp.concatenate(
        [
            jnp.einsum("pq,pqs->ps", weight, f.astype(jnp.float32), precision=lax.Precision.HIGHEST)
            for f in level_parts
        ],
        axis=1,
    )


def solution(mesh):
    return jax.shard_map(
        per_device,
        mesh=mesh,
        in_specs=(P("fold", "blk"), P(None, "fold"), P()),
        out_specs=P("blk", "fold"),
        check_vma=False,
    )
```

```python
import jax
import jax.numpy as jnp
from jax import lax
from jax.experimental import pallas as pl
from jax.sharding import PartitionSpec as P

B = 512
ITERS = 8


LAMBDAS = (0.2, 2.0)
LEVEL_ONE = 0.1
EPSILON = 1e-06


def chebyshev(times_system, target, low_edge, high_edge):
    center = 0.5 * (high_edge + low_edge)
    radius = 0.5 * (high_edge - low_edge)
    sigma_ratio = center / radius
    rho_now = 1.0 / sigma_ratio
    direction = target / center
    solution = jnp.zeros_like(target)
    residual = target
    for iteration in range(ITERS):
        solution = solution + direction
        if iteration + 1 < ITERS:
            residual = residual - times_system(direction)
            rho_next = 1.0 / (2.0 * sigma_ratio - rho_now)
            direction = rho_next * rho_now * direction + 2.0 * rho_next / radius * residual
            rho_now = rho_next
    return solution


def _spd_solve_kernel(a_ref, b_ref, w_ref):
    a = a_ref[...]
    b = b_ref[...]
    t, q, _ = a.shape
    rowi = lax.broadcasted_iota(jnp.int32, (t, q, 1), 1)
    coli = lax.broadcasted_iota(jnp.int32, (t, 1, q), 2)
    y = jnp.zeros_like(b)
    columns = []
    for k in range(q):
        s = jnp.sqrt(a[:, k:k + 1, k:k + 1])
        lcol = jnp.where(rowi == k, s, jnp.where(rowi > k, a[:, :, k:k + 1] / s, 0.0))
        lrow = jnp.where(coli == k, s, jnp.where(coli > k, a[:, k:k + 1, :] / s, 0.0))
        a = a - lcol * lrow
        yk = b[:, k:k + 1, :] / s
        b = b - jnp.where(rowi > k, lcol * yk, 0.0)
        y = jnp.where(rowi == k, yk, y)
        columns.append(lcol)
    w = jnp.zeros_like(b)
    for k in reversed(range(q)):
        lcol = columns[k]
        acc = jnp.sum(jnp.where(rowi > k, lcol * w, 0.0), axis=1, keepdims=True)
        w = jnp.where(rowi == k, (y[:, k:k + 1, :] - acc) / lcol[:, k:k + 1, :], w)
    w_ref[...] = w


def spd_solve(a, b):
    return pl.pallas_call(
        _spd_solve_kernel,
        out_shape=jax.ShapeDtypeStruct(b.shape, jnp.float32),
    )(a, b)


def butterfly_sum(x, axis):
    n = lax.axis_size(axis)
    if n & (n - 1):
        return lax.psum(x, axis)
    stride = 1
    while stride < n:
        radix = min(4, n // stride)
        total = x
        for shift in range(1, radix):
            perm = []
            for i in range(n):
                digit = (i // stride) % radix
                perm.append((i, i + ((digit + shift) % radix - digit) * stride))
            total = total + lax.ppermute(x, axis, perm)
        x = total
        stride *= radix
    return x


def exchange_sum(arrays, axis):
    n = lax.axis_size(axis)
    flat = jnp.concatenate([a.reshape(-1) for a in arrays])
    size = flat.shape[0]
    unit = n * 8 * 128
    flat = jnp.pad(flat, (0, -(-size // unit) * unit - size))
    pieces = lax.all_to_all(flat.reshape(n, -1, 128), axis, 0, 0, tiled=True)
    chunk = jnp.sum(pieces, axis=0)
    whole = lax.all_to_all(jnp.broadcast_to(chunk[None], (n,) + chunk.shape), axis, 0, 0, tiled=True)
    whole = whole.reshape(-1)
    out = []
    offset = 0
    for a in arrays:
        out.append(whole[offset:offset + a.size].reshape(a.shape))
        offset += a.size
    return out


def per_device(genotypes, phenotypes, trait_order):
    n_fold = lax.axis_size("fold")
    sample_rows = genotypes.shape[0]
    block_count = genotypes.shape[1] // B
    total_rows = sample_rows * n_fold
    held_rows = float(total_rows - sample_rows)
    phen = jnp.take(phenotypes, trait_order, axis=0)
    p_size = phen.shape[0]
    half = B // 2
    rows = lax.broadcasted_iota(jnp.int32, (half, half), 0)
    cols = lax.broadcasted_iota(jnp.int32, (half, half), 1)
    eye_h = rows == cols

    def pack(gram):
        a11, a12, a22 = gram[:half, :half], gram[:half, half:], gram[half:, half:]
        tile = jnp.where(rows > cols, a11, a22)
        diag = jnp.sum(jnp.where(eye_h, a11, 0.0), axis=1)
        return jnp.concatenate([a12, tile, diag[None]], axis=0)

    def unpack(packed):
        a12, tile, diag = packed[:half], packed[half:B], packed[B]
        tile_t = tile.T
        a22 = jnp.where(rows <= cols, tile, tile_t)
        a11 = jnp.where(rows > cols, tile, jnp.where(rows < cols, tile_t, jnp.where(eye_h, diag[:, None], 0.0)))
        top = jnp.concatenate([a11, a12], axis=1)
        bottom = jnp.concatenate([a12.T, a22], axis=1)
        return jnp.concatenate([top, bottom], axis=0)

    gram_parts = []
    early_totals = []
    for b in range(block_count):
        xb = genotypes[:, b * B:(b + 1) * B]
        gram_parts.append(jnp.einsum("si,sj->ij", xb, xb, preferred_element_type=jnp.float32))
        if b + 1 < block_count:
            early_totals += exchange_sum([pack(gram_parts[-1])], "fold")
    phen_aug = jnp.concatenate([phen, jnp.ones((1, sample_rows), phen.dtype)], axis=0)
    cross_aug = jnp.dot(phen_aug, genotypes, preferred_element_type=jnp.float32)
    phen_local = jnp.sum(phen.astype(jnp.float32), axis=1)
    phen_row = jnp.zeros((1, genotypes.shape[1]), jnp.float32).at[0, :p_size].set(phen_local)
    sums_local = jnp.concatenate([cross_aug, phen_row], axis=0)
    totals = early_totals + exchange_sum([pack(gram_parts[-1]), sums_local], "fold")
    sums_total = totals[-1]
    gram_part = jnp.stack(gram_parts)
    gram_sum = jnp.stack([unpack(p) for p in totals[:-1]])
    phen_total = sums_total[p_size + 1, :p_size]
    cross_aug = cross_aug.reshape(p_size + 1, block_count, B)
    cross_aug_total = sums_total[: p_size + 1].reshape(p_size + 1, block_count, B)
    cross_local = jnp.transpose(cross_aug[:p_size], (1, 0, 2))
    col_local = cross_aug[p_size]
    cross_total = jnp.transpose(cross_aug_total[:p_size], (1, 0, 2))
    col_total = cross_aug_total[p_size]
    mean_dose = col_total / total_rows
    eye = jnp.eye(B, dtype=jnp.bool_)
    gram_diag = jnp.sum(jnp.where(eye[None], gram_sum, 0.0), axis=2)
    inv_scale = 1.0 / jnp.sqrt(gram_diag / total_rows - mean_dose * mean_dose + EPSILON)
    gram_out = gram_sum - gram_part
    col_out = col_total - col_local
    cross_out = cross_total - cross_local
    phen_out = phen_total - phen_local
    centered = (
        gram_out
        - col_out[:, :, None] * mean_dose[:, None, :]
        - mean_dose[:, :, None] * col_out[:, None, :]
        + held_rows * mean_dose[:, :, None] * mean_dose[:, None, :]
    )
    system = inv_scale[:, :, None] * centered * inv_scale[:, None, :] / held_rows
    target = (
        (cross_out - phen_out[None, :, None] * mean_dose[:, None, :])
        * inv_scale[:, None, :]
        / held_rows
    )
    bound = jnp.max(jnp.sum(jnp.abs(system), axis=2), axis=1)
    penalty = jnp.array(LAMBDAS, jnp.float32)
    low_edge = jnp.broadcast_to(penalty[None, :, None, None], (block_count, penalty.shape[0], 1, 1))
    high_edge = low_edge + bound[:, None, None, None]

    def times_system(direction):
        return (
            jnp.einsum(
                "brpi,bij->brpj",
                direction,
                system,
                precision=lax.Precision.HIGH,
                preferred_element_type=jnp.float32,
            )
            + low_edge * direction
        )

    stacked = jnp.broadcast_to(target[:, None], (block_count, penalty.shape[0]) + target.shape[1:])
    coef = chebyshev(times_system, stacked, low_edge, high_edge)
    scaled = (inv_scale[:, None, None, :] * coef).astype(jnp.bfloat16)
    offset = jnp.einsum(
        "bi,brpi->pbr", mean_dose, scaled.astype(jnp.float32), precision=lax.Precision.HIGH
    )
    halves = 2
    part_rows = sample_rows // halves
    blk_index = lax.axis_index("blk")
    level_parts = []
    hgram_own = 0.0
    hcross_own = 0.0
    for h in range(halves):
        rows_h = slice(h * part_rows, (h + 1) * part_rows)
        product = jnp.stack(
            [
                jnp.einsum(
                    "si,rpi->prs",
                    genotypes[rows_h, b * B:(b + 1) * B],
                    scaled[b],
                    preferred_element_type=jnp.float32,
                )
                for b in range(block_count)
            ],
            axis=1,
        )
        feature = (product - offset[:, :, :, None]).astype(jnp.bfloat16)
        owned = lax.all_to_all(feature, "blk", split_axis=0, concat_axis=1, tiled=True)
        own_traits = owned.shape[0]
        feature_count = owned.shape[1] * owned.shape[2]
        level_feat = owned.reshape(own_traits, feature_count, part_rows)
        target_own = lax.dynamic_slice_in_dim(phen[:, rows_h], blk_index * own_traits, own_traits, 0)
        hgram_own = hgram_own + jnp.einsum(
            "pqs,pts->pqt", level_feat, level_feat, preferred_element_type=jnp.float32
        )
        hcross_own = hcross_own + jnp.einsum(
            "pqs,ps->pq", level_feat, target_own, preferred_element_type=jnp.float32
        )
        level_parts.append(level_feat)
    level_own = jnp.concatenate([hgram_own, hcross_own[:, :, None]], axis=2)
    level_total = butterfly_sum(level_own, "fold")
    hgram_total = level_total[:, :, :feature_count]
    hcross_total = level_total[:, :, feature_count]
    hgram_out = hgram_total - hgram_own
    hcross_out = hcross_total - hcross_own
    trace_sum = jnp.trace(hgram_out, axis1=1, axis2=2)
    level_system = hgram_out / held_rows + (LEVEL_ONE * trace_sum / (held_rows * feature_count))[
        :, None, None
    ] * jnp.eye(feature_count, dtype=jnp.float32)
    weight = spd_solve(level_system, (hcross_out / held_rows)[:, :, None])[:, :, 0]
    return jnp.concatenate(
        [
            jnp.einsum("pq,pqs->ps", weight, f.astype(jnp.float32), precision=lax.Precision.HIGH)
            for f in level_parts
        ],
        axis=1,
    )


def solution(mesh):
    return jax.shard_map(
        per_device,
        mesh=mesh,
        in_specs=(P("fold", "blk"), P(None, "fold"), P()),
        out_specs=P("blk", "fold"),
        check_vma=False,
    )
```
